128 devices in a mesh: pairs: 16 (over z_hi, x, core), band: 8 (over y, z_lo).
Axes of the slice: x: 4, y: 4, z: 4 (z_hi: 2, z_lo: 2; z = z_hi * 2 + z_lo), core: 2. Of those that a mesh axis runs over, the one named last changes fastest.
Arguments:
- spectra: bfloat16 [8192, 8, 1024], P('pairs', 'band'), may hold values from -15 to 15
- observed: bfloat16 [32768, 8, 1024], P('pairs', 'band'), may hold values from -5 to 5
- pair_owner: int32 [32768, 2], P('pairs'), may hold values from 0 to 15, all different within a row; in each aligned block of 2048 rows (0 to 2047, 2048 to 4095, ...) at most 384 rows name the same one
- pair_slot: int32 [32768, 2], P('pairs'), may hold values from 0 to 511
- win_start: int32 [32768], P('pairs'), may hold values from 0 to 511
- win_end: int32 [32768], P('pairs'), may hold values from 513 to 1024
Outputs:
- noise_kernel: float32 [8192, 8, 512], P('pairs', 'band')
The draws below stay inside these ranges and needn't reach their ends.
Inputs may be any that keep to these rules, and one draw needn't show every extreme that they name: `pair_owner`: the two stations of a pair have different owners; among the pairs of one index of pairs no owner is named more than 384 times, a bound that some block reaches.
All inputs are finite; a program needn't handle non-finite values.
Results may differ from the reference program's by a relative error of at most 0.006.
Values may be sent and summed in bfloat16 or wider, within the bound.
No kernel may reach another device: no remote copies, remote signals or barrier semaphores. Data moves between devices by JAX's collectives and lax.ppermute only.
A program may use at most 128 MiB of HBM per device.

```python
import math
import jax
import jax.numpy as jnp
import numpy as np
from jax import lax

F = 512
LAGS = 1024
STA_DEV = 512
P_DEV = 2048
CAP = 384
STATIONS = 8192
BANDS = 8
PAIRS = 32768
N_PAIRS = 16


def draw_spectra(key, part):
    key_base, key_scale = jax.random.split(jax.random.fold_in(key, 17))
    base = jnp.clip(jax.random.normal(key_base, (STATIONS, BANDS, 2 * F), jnp.float32), -5.0, 5.0)
    station_scale = jnp.exp(jax.random.uniform(key_scale, (STATIONS, 1, 1), jnp.float32, math.log(0.3), math.log(3.0)))
    falloff = jnp.exp(-math.log(3.0) * jnp.arange(BANDS, dtype=jnp.float32) / max(BANDS - 1, 1))[None, :, None]
    return (base * station_scale * falloff).astype(jnp.bfloat16)


def touch_ends(drawn, rng, least, high):
    longest = drawn.shape.index(max(drawn.shape))
    spots = []
    for shift in (0, 1):
        where = [jax.random.randint(jax.random.fold_in(rng, axis), (), 0, length) for axis, length in enumerate(drawn.shape)]
        where[longest] = (where[longest] + shift) % drawn.shape[longest]
        spots.append(tuple(where))
    return drawn.at[spots[0]].set(least).at[spots[1]].set(high)


def levels(own_key, shape, cuts, least, high):
    gain, own = 1.0, jax.random.fold_in(own_key, 6)
    for axis_at, blocks in cuts:
        draws = jnp.exp(jax.random.uniform(jax.random.fold_in(own, axis_at), (blocks,), jnp.float32, least / len(cuts), high / len(cuts)))
        gain = gain * jnp.repeat(draws, shape[axis_at] // blocks).reshape([-1 if axis == axis_at else 1 for axis in range(len(shape))])
    return gain


def deal_out(rng, own, number, rows, number_of, top, limit, skew):
    order = jax.random.permutation(rng, number_of)
    packed, common = shares(number_of, rows * top, limit, skew, True), shares(number_of, rows * top, limit, skew, False)
    places = jnp.arange(number_of)

    def named(sizes, offset_by):
        used = int((sizes > 0).sum())
        fixed = max(1, used // 4)
        shifted = fixed + (places - fixed + offset_by * (used - fixed)) % max(1, number_of - fixed)
        return jnp.zeros((number_of,), jnp.int32).at[order[jnp.where(places < fixed, places, shifted)]].set(jnp.asarray(sizes, jnp.int32))

    sizes = jnp.where(number % 4 == 0, named(packed, number // 4), named(common, number - number // 4 - 1))
    mixed = jax.random.permutation(jax.random.fold_in(own, 3), number_of)
    source_of, taker = mixed[0:number_of // 2 * 2:2], mixed[1:number_of // 2 * 2:2]
    room = jnp.minimum(sizes[source_of] - 1, limit - sizes[taker]) // 2
    room = jnp.where((source_of == order[0]) | (taker == order[0]) | (sizes[taker] == 0), 0, jnp.maximum(room, 0))
    shifted = jax.random.randint(jax.random.fold_in(own, 4), (number_of // 2,), 0, 1 << 20) % (room + 1)
    sizes = sizes.at[source_of].add(-shifted).at[taker].add(shifted)
    members = jnp.searchsorted(jnp.cumsum(sizes), jnp.arange(rows * top), side="right").astype(jnp.int32)
    grid = members.reshape(top, rows).T
    grid = grid[jax.random.permutation(jax.random.fold_in(own, 1), rows)]
    offset_by = jax.random.randint(jax.random.fold_in(own, 2), (rows, 1), 0, top)
    return jnp.take_along_axis(grid, (jnp.arange(top)[None, :] + offset_by) % top, axis=1)


def shares(amount, total, bound, lean, full):
    portions = [(1 << 20) // math.isqrt(grade ** lean) + 1 for grade in range(1, amount + 1)]
    largest = bound if full else min(bound, max(-(-total // amount), total * portions[0] // sum(portions)))
    least = 1 if total - largest >= amount - 1 else 0
    counts, surplus = [largest] + [least] * (amount - 1), total - largest - least * (amount - 1)
    while surplus > 0:
        candidates = [i for i in range(1, amount) if counts[i] < largest] or [i for i in range(1, amount) if counts[i] < bound]
        whole, left = sum([portions[i] for i in candidates]), surplus
        for i in candidates:
            more = min(bound - counts[i], max(1, left * portions[i] // whole), surplus)
            counts[i] = counts[i] + more
            surplus = surplus - more
    return np.array(counts)


def normal_values(own_key, shape, scale, most, cuts=(), kind=jnp.bfloat16):
    drawn = scale * jax.random.normal(own_key, shape, jnp.float32)
    if cuts:
        drawn = drawn * levels(own_key, shape, cuts, -0.22, 0.18)
    return jnp.clip(drawn, -most, most).astype(kind)


def setup_inputs(seed: int = 0) -> dict:
    streams_of = jax.random.split(jax.random.key(seed), 7)
    spectra = draw_spectra(jax.random.fold_in(streams_of[6], 71), 0)
    observed = normal_values(streams_of[1], (PAIRS, BANDS, LAGS), 0.7, 5.0, ((0, 16), (1, 8)))
    pair_owner_keys = jax.random.split(jax.random.fold_in(streams_of[2], 1), PAIRS // P_DEV)
    pair_owner_turns = jax.random.permutation(jax.random.fold_in(streams_of[2], 3), PAIRS // P_DEV)
    pair_owner = jax.vmap(lambda own, number: deal_out(jax.random.fold_in(streams_of[2], 2), own, number, P_DEV, N_PAIRS, 2, CAP, 2))(pair_owner_keys, pair_owner_turns).reshape((PAIRS, 2))
    pair_slot = touch_ends(jax.random.randint(streams_of[3], (PAIRS, 2), 0, STA_DEV), jax.random.fold_in(streams_of[3], 1), 0, STA_DEV - 1).astype(jnp.int32)
    win_start = touch_ends(jax.random.randint(streams_of[4], (PAIRS,), 0, LAGS // 2), jax.random.fold_in(streams_of[4], 1), 0, (LAGS // 2) - 1).astype(jnp.int32)
    win_end = touch_ends(jax.random.randint(streams_of[5], (PAIRS,), LAGS // 2 + 1, LAGS + 1), jax.random.fold_in(streams_of[5], 1), LAGS // 2 + 1, LAGS).astype(jnp.int32)
    return {"spectra": spectra, "observed": observed, "pair_owner": pair_owner, "pair_slot": pair_slot, "win_start": win_start, "win_end": win_end}


def lag_basis(half_width, lag_count):
    freqs = jnp.arange(half_width, dtype=jnp.int32)
    lag_index = jnp.arange(lag_count, dtype=jnp.int32)
    phases = (freqs[:, None] * lag_index[None, :] % lag_count).astype(jnp.float32) * (2.0 * math.pi / lag_count)
    factor = 1.0 / math.sqrt(lag_count)
    return jnp.concatenate([jnp.cos(phases) * factor, -jnp.sin(phases) * factor], axis=0).astype(jnp.bfloat16)

def reference(spectra, observed, pair_owner, pair_slot, win_start, win_end):
    spectrum = spectra.astype(jnp.float32)
    powers = lax.optimization_barrier(jnp.sum(spectrum * spectrum, axis=(1, 2))) / (BANDS * 2 * F)
    whitened = (spectrum * lax.rsqrt(powers + 1e-05)[:, None, None]).astype(jnp.bfloat16)
    endpoints = (pair_owner * STA_DEV + pair_slot).astype(jnp.int32)
    table = lag_basis(F, LAGS)
    lag_index = jnp.arange(LAGS, dtype=jnp.int32)
    window = ((lag_index[None, :] >= win_start[:, None]) & (lag_index[None, :] < win_end[:, None])).astype(jnp.float32)
    slot_ids = jnp.concatenate([endpoints[:, 0], endpoints[:, 1]])

    def one_band(band_index):
        band_spec = whitened[:, band_index, :]
        near_end = band_spec[endpoints[:, 0]].astype(jnp.float32)
        far_end = band_spec[endpoints[:, 1]].astype(jnp.float32)
        near_re, near_im = (near_end[:, :F], near_end[:, F:])
        far_re, far_im = (far_end[:, :F], far_end[:, F:])
        cross_spec = jnp.concatenate([near_re * far_re + near_im * far_im, near_im * far_re - near_re * far_im], axis=1).astype(jnp.bfloat16)
        lagged = jnp.dot(cross_spec, table, preferred_element_type=jnp.float32)
        observed_band = observed[:, band_index, :].astype(jnp.float32)
        residual = (window * (lagged - observed_band)).astype(jnp.bfloat16)
        adjoint = jnp.dot(residual, table.T, preferred_element_type=jnp.float32)
        adj_re, adj_im = (adjoint[:, :F], adjoint[:, F:])
        to_first = jnp.concatenate([adj_re * far_re - adj_im * far_im, adj_re * far_im + adj_im * far_re], axis=1).astype(jnp.bfloat16)
        to_second = jnp.concatenate([adj_re * near_re + adj_im * near_im, adj_re * near_im - adj_im * near_re], axis=1).astype(jnp.bfloat16)
        contribs = jnp.concatenate([to_first, to_second], axis=0).astype(jnp.float32)
        summed = jax.ops.segment_sum(contribs, slot_ids, num_segments=STATIONS)
        own_spec = band_spec.astype(jnp.float32)
        return 0.25 * (summed[:, :F] * own_spec[:, :F] + summed[:, F:] * own_spec[:, F:])
    kernels = lax.map(one_band, jnp.arange(BANDS, dtype=jnp.int32))
    return jnp.transpose(kernels, (1, 0, 2))
```

```python
import math

import jax
import jax.numpy as jnp
from jax import lax
from jax.sharding import PartitionSpec as P


def lag_basis(half_width, lag_count):
    freqs = jnp.arange(half_width, dtype=jnp.int32)
    lag_index = jnp.arange(lag_count, dtype=jnp.int32)
    phases = (freqs[:, None] * lag_index[None, :] % lag_count).astype(jnp.float32) * (
        2.0 * math.pi / lag_count
    )
    factor = 1.0 / math.sqrt(lag_count)
    return jnp.concatenate([jnp.cos(phases) * factor, -jnp.sin(phases) * factor], axis=0).astype(
        jnp.bfloat16
    )


def owner_positions(owner_flat, owner_count):
    onehot = (owner_flat[:, None] == jnp.arange(owner_count, dtype=jnp.int32)[None, :]).astype(
        jnp.int32
    )
    before = jnp.cumsum(onehot, axis=0) - onehot
    return jnp.sum(before * onehot, axis=1)


def shards(spectra, observed, pair_owner, pair_slot, win_start, win_end):
    owners = lax.axis_size("pairs")
    station_count = spectra.shape[0]
    band_count = spectra.shape[1]
    full_width = spectra.shape[2]
    half_width = full_width // 2
    pair_count = observed.shape[0]
    lag_count = observed.shape[2]
    capacity = 3 * pair_count // owners
    raw = spectra.reshape(station_count, full_width)
    panel_raw = lax.all_gather(raw, "pairs", axis=0, tiled=True)
    spectrum = raw.astype(jnp.float32)
    local_power = jnp.sum(spectrum * spectrum, axis=1)
    total_power = lax.psum(local_power, "band")
    entries = band_count * lax.axis_size("band") * full_width
    scale = lax.rsqrt(total_power / entries + 1e-05)
    own_spec = (spectrum * scale[:, None]).astype(jnp.bfloat16).astype(jnp.float32)
    panel_scale = lax.all_gather(scale, "pairs", axis=0, tiled=True)

    owner_flat = pair_owner.reshape(-1)
    slot_flat = pair_slot.reshape(-1)
    position = owner_positions(owner_flat, owners)
    flat_slot = owner_flat * capacity + position
    request = (
        jnp.full((owners * capacity,), station_count, jnp.int32)
        .at[flat_slot]
        .set(slot_flat, unique_indices=True)
    )
    wanted = lax.all_to_all(
        request.reshape(owners, capacity), "pairs", split_axis=0, concat_axis=0, tiled=True
    ).reshape(owners * capacity)

    rows0 = pair_owner[:, 0] * station_count + pair_slot[:, 0]
    rows1 = pair_owner[:, 1] * station_count + pair_slot[:, 1]
    near_end = panel_raw[rows0].astype(jnp.float32) * panel_scale[rows0][:, None]
    far_end = panel_raw[rows1].astype(jnp.float32) * panel_scale[rows1][:, None]
    near_end = near_end.astype(jnp.bfloat16).astype(jnp.float32)
    far_end = far_end.astype(jnp.bfloat16).astype(jnp.float32)
    near_re, near_im = (near_end[:, :half_width], near_end[:, half_width:])
    far_re, far_im = (far_end[:, :half_width], far_end[:, half_width:])
    cross_spec = jnp.concatenate(
        [near_re * far_re + near_im * far_im, near_im * far_re - near_re * far_im], axis=-1
    ).astype(jnp.bfloat16)
    table = lag_basis(half_width, lag_count)
    lagged = jnp.dot(cross_spec, table, preferred_element_type=jnp.float32)
    lag_index = jnp.arange(lag_count, dtype=jnp.int32)
    window = (lag_index[None, :] >= win_start[:, None]) & (lag_index[None, :] < win_end[:, None])
    obs = observed.reshape(pair_count, lag_count).astype(jnp.float32)
    residual = jnp.where(window, lagged - obs, 0.0).astype(jnp.bfloat16)
    adjoint = lax.dot_general(
        residual, table, (((1,), (1,)), ((), ())), preferred_element_type=jnp.float32
    )
    adj_re, adj_im = (adjoint[:, :half_width], adjoint[:, half_width:])
    to_first = jnp.concatenate(
        [adj_re * far_re - adj_im * far_im, adj_re * far_im + adj_im * far_re], axis=-1
    ).astype(jnp.bfloat16)
    to_second = jnp.concatenate(
        [adj_re * near_re + adj_im * near_im, adj_re * near_im - adj_im * near_re], axis=-1
    ).astype(jnp.bfloat16)
    stacked = jnp.stack([to_first, to_second], axis=1).reshape(2 * pair_count, full_width)
    outgoing = (
        jnp.zeros((owners * capacity, full_width), jnp.bfloat16)
        .at[flat_slot]
        .set(stacked, unique_indices=True)
    )
    incoming = lax.all_to_all(
        outgoing.reshape(owners, capacity, full_width),
        "pairs",
        split_axis=0,
        concat_axis=0,
        tiled=True,
    ).reshape(owners * capacity, full_width)
    onehot = (
        wanted[None, :] == jnp.arange(station_count, dtype=jnp.int32)[:, None]
    ).astype(jnp.bfloat16)
    summed = jnp.dot(onehot, incoming, preferred_element_type=jnp.float32)
    result = 0.25 * (
        summed[:, :half_width] * own_spec[:, :half_width]
        + summed[:, half_width:] * own_spec[:, half_width:]
    )
    return result.reshape(station_count, band_count, half_width)


def solution(mesh):
    return jax.shard_map(
        shards,
        mesh=mesh,
        in_specs=(
            P("pairs", "band", None),
            P("pairs", "band", None),
            P("pairs", None),
            P("pairs", None),
            P("pairs"),
            P("pairs"),
        ),
        out_specs=P("pairs", "band", None),
        check_vma=False,
    )
```

```python
import math

import jax
import jax.numpy as jnp
from jax import lax
from jax.sharding import PartitionSpec as P
from jax.experimental import pallas as pl
from jax.experimental.pallas import tpu as pltpu


def lag_basis(half_width, lag_count):
    freqs = jnp.arange(half_width, dtype=jnp.int32)
    lag_index = jnp.arange(lag_count, dtype=jnp.int32)
    phases = (freqs[:, None] * lag_index[None, :] % lag_count).astype(jnp.float32) * (
        2.0 * math.pi / lag_count
    )
    factor = 1.0 / math.sqrt(lag_count)
    return jnp.concatenate([jnp.cos(phases) * factor, -jnp.sin(phases) * factor], axis=0).astype(
        jnp.bfloat16
    )


def owner_positions(owner_flat, owner_count):
    onehot = (owner_flat[:, None] == jnp.arange(owner_count, dtype=jnp.int32)[None, :]).astype(
        jnp.int32
    )
    before = jnp.cumsum(onehot, axis=0) - onehot
    return jnp.sum(before * onehot, axis=1)


def round_bf16(x):
    return x.astype(jnp.bfloat16).astype(jnp.float32)


def pair_kernel(near_ref, far_ref, ns_ref, fs_ref, obs_ref, ws_ref, we_ref, table_ref, out_ref):
    half = near_ref.shape[1] // 2
    near = round_bf16(near_ref[...].astype(jnp.float32) * ns_ref[...])
    far = round_bf16(far_ref[...].astype(jnp.float32) * fs_ref[...])
    near_re, near_im = near[:, :half], near[:, half:]
    far_re, far_im = far[:, :half], far[:, half:]
    cross_re = (near_re * far_re + near_im * far_im).astype(jnp.bfloat16)
    cross_im = (near_im * far_re - near_re * far_im).astype(jnp.bfloat16)
    tab_re = table_ref[:half, :]
    tab_im = table_ref[half:, :]
    lagged = jnp.dot(cross_re, tab_re, preferred_element_type=jnp.float32) + jnp.dot(
        cross_im, tab_im, preferred_element_type=jnp.float32
    )
    lag = lax.broadcasted_iota(jnp.int32, lagged.shape, 1)
    inside = (lag >= ws_ref[...]) & (lag < we_ref[...])
    residual = jnp.where(inside, lagged - obs_ref[...].astype(jnp.float32), 0.0).astype(
        jnp.bfloat16
    )
    dims = (((1,), (1,)), ((), ()))
    adj_re = lax.dot_general(residual, tab_re, dims, preferred_element_type=jnp.float32)
    adj_im = lax.dot_general(residual, tab_im, dims, preferred_element_type=jnp.float32)
    out_ref[0, :, :half] = (adj_re * far_re - adj_im * far_im).astype(jnp.bfloat16)
    out_ref[0, :, half:] = (adj_re * far_im + adj_im * far_re).astype(jnp.bfloat16)
    out_ref[1, :, :half] = (adj_re * near_re + adj_im * near_im).astype(jnp.bfloat16)
    out_ref[1, :, half:] = (adj_re * near_im - adj_im * near_re).astype(jnp.bfloat16)


def pair_contributions(near_raw, far_raw, near_scale, far_scale, obs, ws, we, table, block=256):
    pairs, width = near_raw.shape
    lags = obs.shape[1]
    row = lambda i: (i, 0)
    return pl.pallas_call(
        pair_kernel,
        grid=(pairs // block,),
        in_specs=[
            pl.BlockSpec((block, width), row),
            pl.BlockSpec((block, width), row),
            pl.BlockSpec((block, 1), row),
            pl.BlockSpec((block, 1), row),
            pl.BlockSpec((block, lags), row),
            pl.BlockSpec((block, 1), row),
            pl.BlockSpec((block, 1), row),
            pl.BlockSpec((width, lags), lambda i: (0, 0)),
        ],
        out_specs=pl.BlockSpec((2, block, width), lambda i: (0, i, 0)),
        out_shape=jax.ShapeDtypeStruct((2, pairs, width), jnp.bfloat16),
        compiler_params=pltpu.CompilerParams(vmem_limit_bytes=48 * 1024 * 1024),
    )(near_raw, far_raw, near_scale, far_scale, obs, ws, we, table)


def shards(spectra, observed, pair_owner, pair_slot, win_start, win_end):
    owners = lax.axis_size("pairs")
    station_count = spectra.shape[0]
    band_count = spectra.shape[1]
    full_width = spectra.shape[2]
    half_width = full_width // 2
    pair_count = observed.shape[0]
    lag_count = observed.shape[2]
    capacity = 3 * pair_count // owners
    raw = spectra.reshape(station_count, full_width)
    panel_raw = lax.all_gather(raw, "pairs", axis=0, tiled=True)
    spectrum = raw.astype(jnp.float32)
    local_power = jnp.sum(spectrum * spectrum, axis=1)
    total_power = lax.psum(local_power, "band")
    entries = band_count * lax.axis_size("band") * full_width
    scale = lax.rsqrt(total_power / entries + 1e-05)
    own_spec = lax.reduce_precision(spectrum * scale[:, None], exponent_bits=8, mantissa_bits=7)
    panel_scale = lax.all_gather(scale, "pairs", axis=0, tiled=True)

    owner_flat = jnp.concatenate([pair_owner[:, 0], pair_owner[:, 1]])
    slot_flat = jnp.concatenate([pair_slot[:, 0], pair_slot[:, 1]])
    position = owner_positions(owner_flat, owners)
    flat_slot = owner_flat * capacity + position
    request = (
        jnp.full((owners * capacity,), station_count, jnp.int32)
        .at[flat_slot]
        .set(slot_flat, unique_indices=True)
    )
    wanted = lax.all_to_all(
        request.reshape(owners, capacity), "pairs", split_axis=0, concat_axis=0, tiled=True
    ).reshape(owners * capacity)

    rows0 = pair_owner[:, 0] * station_count + pair_slot[:, 0]
    rows1 = pair_owner[:, 1] * station_count + pair_slot[:, 1]
    near_raw = panel_raw[rows0]
    far_raw = panel_raw[rows1]
    near_scale = panel_scale[rows0][:, None]
    far_scale = panel_scale[rows1][:, None]
    table = lag_basis(half_width, lag_count)
    obs = observed.reshape(pair_count, lag_count)
    contribs = pair_contributions(
        near_raw, far_raw, near_scale, far_scale, obs,
        win_start[:, None], win_end[:, None], table,
    ).reshape(2 * pair_count, full_width)
    outgoing = (
        jnp.zeros((owners * capacity, full_width), jnp.bfloat16)
        .at[flat_slot]
        .set(contribs, unique_indices=True)
    )
    incoming = lax.all_to_all(
        outgoing.reshape(owners, capacity, full_width),
        "pairs",
        split_axis=0,
        concat_axis=0,
        tiled=True,
    ).reshape(owners * capacity, full_width)
    onehot = (
        wanted[None, :] == jnp.arange(station_count, dtype=jnp.int32)[:, None]
    ).astype(jnp.bfloat16)
    summed = jnp.dot(onehot, incoming, preferred_element_type=jnp.float32)
    result = 0.25 * (
        summed[:, :half_width] * own_spec[:, :half_width]
        + summed[:, half_width:] * own_spec[:, half_width:]
    )
    return result.reshape(station_count, band_count, half_width)


def solution(mesh):
    return jax.shard_map(
        shards,
        mesh=mesh,
        in_specs=(
            P("pairs", "band", None),
            P("pairs", "band", None),
            P("pairs", None),
            P("pairs", None),
            P("pairs"),
            P("pairs"),
        ),
        out_specs=P("pairs", "band", None),
        check_vma=False,
    )
```

```python
import math

import jax
import jax.numpy as jnp
from jax import lax
from jax.sharding import PartitionSpec as P
from jax.experimental import pallas as pl
from jax.experimental.pallas import tpu as pltpu


def lag_basis(half_width, lag_count):
    freqs = jnp.arange(half_width, dtype=jnp.int32)
    lag_index = jnp.arange(lag_count, dtype=jnp.int32)
    phases = (freqs[:, None] * lag_index[None, :] % lag_count).astype(jnp.float32) * (
        2.0 * math.pi / lag_count
    )
    factor = 1.0 / math.sqrt(lag_count)
    return jnp.concatenate([jnp.cos(phases) * factor, -jnp.sin(phases) * factor], axis=0).astype(
        jnp.bfloat16
    )


def owner_positions(owner_flat, owner_count):
    onehot = (owner_flat[:, None] == jnp.arange(owner_count, dtype=jnp.int32)[None, :]).astype(
        jnp.int32
    )
    before = jnp.cumsum(onehot, axis=0) - onehot
    return jnp.sum(before * onehot, axis=1)


def round_bf16(x):
    return x.astype(jnp.bfloat16).astype(jnp.float32)


def pair_kernel(
    nr_ref, ni_ref, fr_ref, fi_ref, ns_ref, fs_ref, obs_ref, ws_ref, we_ref, table_ref,
    re_ref, im_ref,
):
    half = nr_ref.shape[1]
    near_re = round_bf16(nr_ref[...].astype(jnp.float32) * ns_ref[...])
    near_im = round_bf16(ni_ref[...].astype(jnp.float32) * ns_ref[...])
    far_re = round_bf16(fr_ref[...].astype(jnp.float32) * fs_ref[...])
    far_im = round_bf16(fi_ref[...].astype(jnp.float32) * fs_ref[...])
    cross_re = (near_re * far_re + near_im * far_im).astype(jnp.bfloat16)
    cross_im = (near_im * far_re - near_re * far_im).astype(jnp.bfloat16)
    tab_re = table_ref[:half, :]
    tab_im = table_ref[half:, :]
    lagged = jnp.dot(cross_re, tab_re, preferred_element_type=jnp.float32) + jnp.dot(
        cross_im, tab_im, preferred_element_type=jnp.float32
    )
    lag = lax.broadcasted_iota(jnp.int32, lagged.shape, 1)
    inside = (lag >= ws_ref[...]) & (lag < we_ref[...])
    residual = jnp.where(inside, lagged - obs_ref[...].astype(jnp.float32), 0.0).astype(
        jnp.bfloat16
    )
    dims = (((1,), (1,)), ((), ()))
    adj_re = lax.dot_general(residual, tab_re, dims, preferred_element_type=jnp.float32)
    adj_im = lax.dot_general(residual, tab_im, dims, preferred_element_type=jnp.float32)
    re_ref[0] = (adj_re * far_re - adj_im * far_im).astype(jnp.bfloat16)
    im_ref[0] = (adj_re * far_im + adj_im * far_re).astype(jnp.bfloat16)
    re_ref[1] = (adj_re * near_re + adj_im * near_im).astype(jnp.bfloat16)
    im_ref[1] = (adj_re * near_im - adj_im * near_re).astype(jnp.bfloat16)


def pair_contributions(rows, near_scale, far_scale, obs, ws, we, table, block=256):
    pairs, half = rows[0].shape
    lags = obs.shape[1]
    row = lambda i: (i, 0)
    half_spec = pl.BlockSpec((block, half), row)
    col_spec = pl.BlockSpec((block, 1), row)
    out_spec = pl.BlockSpec((2, block, half), lambda i: (0, i, 0))
    out_shape = jax.ShapeDtypeStruct((2, pairs, half), jnp.bfloat16)
    return pl.pallas_call(
        pair_kernel,
        grid=(pairs // block,),
        in_specs=[half_spec] * 4
        + [col_spec, col_spec, pl.BlockSpec((block, lags), row), col_spec, col_spec]
        + [pl.BlockSpec((2 * half, lags), lambda i: (0, 0))],
        out_specs=[out_spec, out_spec],
        out_shape=[out_shape, out_shape],
        compiler_params=pltpu.CompilerParams(vmem_limit_bytes=48 * 1024 * 1024),
    )(*rows, near_scale, far_scale, obs, ws, we, table)


def shards(spectra, observed, pair_owner, pair_slot, win_start, win_end):
    owners = lax.axis_size("pairs")
    station_count = spectra.shape[0]
    band_count = spectra.shape[1]
    full_width = spectra.shape[2]
    half_width = full_width // 2
    pair_count = observed.shape[0]
    lag_count = observed.shape[2]
    capacity = 3 * pair_count // owners
    raw = spectra.reshape(station_count, full_width)
    panel_re = lax.all_gather(raw[:, :half_width], "pairs", axis=0, tiled=True)
    panel_im = lax.all_gather(raw[:, half_width:], "pairs", axis=0, tiled=True)
    spectrum = raw.astype(jnp.float32)
    local_power = jnp.sum(spectrum * spectrum, axis=1)
    total_power = lax.psum(local_power, "band")
    entries = band_count * lax.axis_size("band") * full_width
    scale = lax.rsqrt(total_power / entries + 1e-05)
    own_spec = lax.reduce_precision(spectrum * scale[:, None], exponent_bits=8, mantissa_bits=7)
    panel_scale = lax.all_gather(scale, "pairs", axis=0, tiled=True)

    owner_flat = jnp.concatenate([pair_owner[:, 0], pair_owner[:, 1]])
    slot_flat = jnp.concatenate([pair_slot[:, 0], pair_slot[:, 1]])
    position = owner_positions(owner_flat, owners)
    flat_slot = owner_flat * capacity + position
    request = (
        jnp.full((owners * capacity,), station_count, jnp.int32)
        .at[flat_slot]
        .set(slot_flat, unique_indices=True)
    )
    wanted = lax.all_to_all(
        request.reshape(owners, capacity), "pairs", split_axis=0, concat_axis=0, tiled=True
    ).reshape(owners * capacity)

    rows0 = pair_owner[:, 0] * station_count + pair_slot[:, 0]
    rows1 = pair_owner[:, 1] * station_count + pair_slot[:, 1]
    rows = (panel_re[rows0], panel_im[rows0], panel_re[rows1], panel_im[rows1])
    near_scale = panel_scale[rows0][:, None]
    far_scale = panel_scale[rows1][:, None]
    table = lag_basis(half_width, lag_count)
    obs = observed.reshape(pair_count, lag_count)
    contrib_re, contrib_im = pair_contributions(
        rows, near_scale, far_scale, obs, win_start[:, None], win_end[:, None], table
    )

    def send(contrib):
        outgoing = (
            jnp.zeros((owners * capacity, half_width), jnp.bfloat16)
            .at[flat_slot]
            .set(contrib.reshape(2 * pair_count, half_width), unique_indices=True)
        )
        return lax.all_to_all(
            outgoing.reshape(owners, capacity, half_width),
            "pairs",
            split_axis=0,
            concat_axis=0,
            tiled=True,
        ).reshape(owners * capacity, half_width)

    incoming_re = send(contrib_re)
    incoming_im = send(contrib_im)
    onehot = (
        wanted[None, :] == jnp.arange(station_count, dtype=jnp.int32)[:, None]
    ).astype(jnp.bfloat16)
    summed_re = jnp.dot(onehot, incoming_re, preferred_element_type=jnp.float32)
    summed_im = jnp.dot(onehot, incoming_im, preferred_element_type=jnp.float32)
    result = 0.25 * (
        summed_re * own_spec[:, :half_width] + summed_im * own_spec[:, half_width:]
    )
    return result.reshape(station_count, band_count, half_width)


def solution(mesh):
    return jax.shard_map(
        shards,
        mesh=mesh,
        in_specs=(
            P("pairs", "band", None),
            P("pairs", "band", None),
            P("pairs", None),
            P("pairs", None),
            P("pairs"),
            P("pairs"),
        ),
        out_specs=P("pairs", "band", None),
        check_vma=False,
    )
```

```python
import math

import jax
import jax.numpy as jnp
from jax import lax
from jax.sharding import PartitionSpec as P
from jax.experimental import pallas as pl
from jax.experimental.pallas import tpu as pltpu


def lag_basis(half_width, lag_count):
    freqs = jnp.arange(half_width, dtype=jnp.int32)
    lag_index = jnp.arange(lag_count, dtype=jnp.int32)
    phases = (freqs[:, None] * lag_index[None, :] % lag_count).astype(jnp.float32) * (
        2.0 * math.pi / lag_count
    )
    factor = 1.0 / math.sqrt(lag_count)
    return jnp.concatenate([jnp.cos(phases) * factor, -jnp.sin(phases) * factor], axis=0).astype(
        jnp.bfloat16
    )


def owner_positions(owner_flat, owner_count):
    onehot = (owner_flat[:, None] == jnp.arange(owner_count, dtype=jnp.int32)[None, :]).astype(
        jnp.int32
    )
    before = jnp.cumsum(onehot, axis=0) - onehot
    return jnp.sum(before * onehot, axis=1)


def round_bf16(x):
    return x.astype(jnp.bfloat16).astype(jnp.float32)


def pair_kernel(near_ref, far_ref, ns_ref, fs_ref, obs_ref, ws_ref, we_ref, table_ref, out_ref):
    half = near_ref.shape[1] // 2
    near = round_bf16(near_ref[...].astype(jnp.float32) * ns_ref[...])
    far = round_bf16(far_ref[...].astype(jnp.float32) * fs_ref[...])
    near_re, near_im = near[:, :half], near[:, half:]
    far_re, far_im = far[:, :half], far[:, half:]
    cross_re = (near_re * far_re + near_im * far_im).astype(jnp.bfloat16)
    cross_im = (near_im * far_re - near_re * far_im).astype(jnp.bfloat16)
    tab_re = table_ref[:half, :]
    tab_im = table_ref[half:, :]
    lagged = jnp.dot(cross_re, tab_re, preferred_element_type=jnp.float32) + jnp.dot(
        cross_im, tab_im, preferred_element_type=jnp.float32
    )
    lag = lax.broadcasted_iota(jnp.int32, lagged.shape, 1)
    inside = (lag >= ws_ref[...]) & (lag < we_ref[...])
    residual = jnp.where(inside, lagged - obs_ref[...].astype(jnp.float32), 0.0).astype(
        jnp.bfloat16
    )
    dims = (((1,), (1,)), ((), ()))
    adj_re = lax.dot_general(residual, tab_re, dims, preferred_element_type=jnp.float32)
    adj_im = lax.dot_general(residual, tab_im, dims, preferred_element_type=jnp.float32)
    out_ref[0, :, :half] = (adj_re * far_re - adj_im * far_im).astype(jnp.bfloat16)
    out_ref[0, :, half:] = (adj_re * far_im + adj_im * far_re).astype(jnp.bfloat16)
    out_ref[1, :, :half] = (adj_re * near_re + adj_im * near_im).astype(jnp.bfloat16)
    out_ref[1, :, half:] = (adj_re * near_im - adj_im * near_re).astype(jnp.bfloat16)


def pair_contributions(near_raw, far_raw, near_scale, far_scale, obs, ws, we, table, block=256):
    pairs, width = near_raw.shape
    lags = obs.shape[1]
    row = lambda i: (i, 0)
    return pl.pallas_call(
        pair_kernel,
        grid=(pairs // block,),
        in_specs=[
            pl.BlockSpec((block, width), row),
            pl.BlockSpec((block, width), row),
            pl.BlockSpec((block, 1), row),
            pl.BlockSpec((block, 1), row),
            pl.BlockSpec((block, lags), row),
            pl.BlockSpec((block, 1), row),
            pl.BlockSpec((block, 1), row),
            pl.BlockSpec((width, lags), lambda i: (0, 0)),
        ],
        out_specs=pl.BlockSpec((2, block, width), lambda i: (0, i, 0)),
        out_shape=jax.ShapeDtypeStruct((2, pairs, width), jnp.bfloat16),
        compiler_params=pltpu.CompilerParams(vmem_limit_bytes=48 * 1024 * 1024),
    )(near_raw, far_raw, near_scale, far_scale, obs, ws, we, table)


def shards(spectra, observed, pair_owner, pair_slot, win_start, win_end):
    owners = lax.axis_size("pairs")
    station_count = spectra.shape[0]
    band_count = spectra.shape[1]
    full_width = spectra.shape[2]
    half_width = full_width // 2
    pair_count = observed.shape[0]
    lag_count = observed.shape[2]
    capacity = 3 * pair_count // owners
    raw = spectra.reshape(station_count, full_width)
    panel_raw = lax.all_gather(raw, "pairs", axis=0, tiled=True)
    spectrum = raw.astype(jnp.float32)
    local_power = jnp.sum(spectrum * spectrum, axis=1)
    total_power = lax.psum(local_power, "band")
    entries = band_count * lax.axis_size("band") * full_width
    scale = lax.rsqrt(total_power / entries + 1e-05)
    own_spec = lax.reduce_precision(spectrum * scale[:, None], exponent_bits=8, mantissa_bits=7)
    panel_scale = lax.all_gather(scale, "pairs", axis=0, tiled=True)

    owner_flat = jnp.concatenate([pair_owner[:, 0], pair_owner[:, 1]])
    slot_flat = jnp.concatenate([pair_slot[:, 0], pair_slot[:, 1]])
    position = owner_positions(owner_flat, owners)
    part = capacity // 2
    flat_slot = (position // part) * (owners * part) + owner_flat * part + position % part
    request = (
        jnp.full((2 * owners * part,), station_count, jnp.int32)
        .at[flat_slot]
        .set(slot_flat, unique_indices=True)
    )
    wanted = lax.all_to_all(
        request.reshape(2, owners, part), "pairs", split_axis=1, concat_axis=1, tiled=True
    ).reshape(2, owners * part)

    rows0 = pair_owner[:, 0] * station_count + pair_slot[:, 0]
    rows1 = pair_owner[:, 1] * station_count + pair_slot[:, 1]
    near_raw = panel_raw[rows0]
    far_raw = panel_raw[rows1]
    near_scale = panel_scale[rows0][:, None]
    far_scale = panel_scale[rows1][:, None]
    table = lag_basis(half_width, lag_count)
    obs = observed.reshape(pair_count, lag_count)
    contribs = pair_contributions(
        near_raw, far_raw, near_scale, far_scale, obs,
        win_start[:, None], win_end[:, None], table,
    ).reshape(2 * pair_count, full_width)
    outgoing = (
        jnp.zeros((2 * owners * part, full_width), jnp.bfloat16)
        .at[flat_slot]
        .set(contribs, unique_indices=True)
    ).reshape(2, owners, part, full_width)
    station_ids = jnp.arange(station_count, dtype=jnp.int32)[:, None]
    summed = None
    for half in range(2):
        incoming = lax.all_to_all(
            outgoing[half], "pairs", split_axis=0, concat_axis=0, tiled=True
        ).reshape(owners * part, full_width)
        onehot = (wanted[half][None, :] == station_ids).astype(jnp.bfloat16)
        partial = jnp.dot(onehot, incoming, preferred_element_type=jnp.float32)
        summed = partial if summed is None else summed + partial
    result = 0.25 * (
        summed[:, :half_width] * own_spec[:, :half_width]
        + summed[:, half_width:] * own_spec[:, half_width:]
    )
    return result.reshape(station_count, band_count, half_width)


def solution(mesh):
    return jax.shard_map(
        shards,
        mesh=mesh,
        in_specs=(
            P("pairs", "band", None),
            P("pairs", "band", None),
            P("pairs", None),
            P("pairs", None),
            P("pairs"),
            P("pairs"),
        ),
        out_specs=P("pairs", "band", None),
        check_vma=False,
    )
```

```python
import math

import jax
import jax.numpy as jnp
from jax import lax
from jax.sharding import PartitionSpec as P
from jax.experimental import pallas as pl
from jax.experimental.pallas import tpu as pltpu


def lag_basis(half_width, lag_count):
    freqs = jnp.arange(half_width, dtype=jnp.int32)
    lag_index = jnp.arange(lag_count, dtype=jnp.int32)
    phases = (freqs[:, None] * lag_index[None, :] % lag_count).astype(jnp.float32) * (
        2.0 * math.pi / lag_count
    )
    factor = 1.0 / math.sqrt(lag_count)
    return jnp.concatenate([jnp.cos(phases) * factor, -jnp.sin(phases) * factor], axis=0).astype(
        jnp.bfloat16
    )


def owner_positions(owner_flat, owner_count):
    onehot = (owner_flat[:, None] == jnp.arange(owner_count, dtype=jnp.int32)[None, :]).astype(
        jnp.int32
    )
    before = jnp.cumsum(onehot, axis=0) - onehot
    return jnp.sum(before * onehot, axis=1)


def round_bf16(x):
    return x.astype(jnp.bfloat16).astype(jnp.float32)


def pair_kernel(near_ref, far_ref, ns_ref, fs_ref, obs_ref, ws_ref, we_ref, table_ref, out_ref):
    half = near_ref.shape[1] // 2
    near = round_bf16(near_ref[...].astype(jnp.float32) * ns_ref[...])
    far = round_bf16(far_ref[...].astype(jnp.float32) * fs_ref[...])
    near_re, near_im = near[:, :half], near[:, half:]
    far_re, far_im = far[:, :half], far[:, half:]
    cross_re = (near_re * far_re + near_im * far_im).astype(jnp.bfloat16)
    cross_im = (near_im * far_re - near_re * far_im).astype(jnp.bfloat16)
    tab_re = table_ref[:half, :]
    tab_im = table_ref[half:, :]
    lagged = jnp.dot(cross_re, tab_re, preferred_element_type=jnp.float32) + jnp.dot(
        cross_im, tab_im, preferred_element_type=jnp.float32
    )
    lag = lax.broadcasted_iota(jnp.int32, lagged.shape, 1)
    inside = (lag >= ws_ref[...]) & (lag < we_ref[...])
    residual = jnp.where(inside, lagged - obs_ref[...].astype(jnp.float32), 0.0).astype(
        jnp.bfloat16
    )
    dims = (((1,), (1,)), ((), ()))
    adj_re = lax.dot_general(residual, tab_re, dims, preferred_element_type=jnp.float32)
    adj_im = lax.dot_general(residual, tab_im, dims, preferred_element_type=jnp.float32)
    out_ref[0, :, :half] = (adj_re * far_re - adj_im * far_im).astype(jnp.bfloat16)
    out_ref[0, :, half:] = (adj_re * far_im + adj_im * far_re).astype(jnp.bfloat16)
    out_ref[1, :, :half] = (adj_re * near_re + adj_im * near_im).astype(jnp.bfloat16)
    out_ref[1, :, half:] = (adj_re * near_im - adj_im * near_re).astype(jnp.bfloat16)


def pair_contributions(near_raw, far_raw, near_scale, far_scale, obs, ws, we, table, block=256):
    pairs, width = near_raw.shape
    lags = obs.shape[1]
    row = lambda i: (i, 0)
    return pl.pallas_call(
        pair_kernel,
        grid=(pairs // block,),
        in_specs=[
            pl.BlockSpec((block, width), row),
            pl.BlockSpec((block, width), row),
            pl.BlockSpec((block, 1), row),
            pl.BlockSpec((block, 1), row),
            pl.BlockSpec((block, lags), row),
            pl.BlockSpec((block, 1), row),
            pl.BlockSpec((block, 1), row),
            pl.BlockSpec((width, lags), lambda i: (0, 0)),
        ],
        out_specs=pl.BlockSpec((2, block, width), lambda i: (0, i, 0)),
        out_shape=jax.ShapeDtypeStruct((2, pairs, width), jnp.bfloat16),
        compiler_params=pltpu.CompilerParams(vmem_limit_bytes=48 * 1024 * 1024),
    )(near_raw, far_raw, near_scale, far_scale, obs, ws, we, table)


def shards(spectra, observed, pair_owner, pair_slot, win_start, win_end):
    owners = lax.axis_size("pairs")
    station_count = spectra.shape[0]
    band_count = spectra.shape[1]
    full_width = spectra.shape[2]
    half_width = full_width // 2
    pair_count = observed.shape[0]
    lag_count = observed.shape[2]
    capacity = 3 * pair_count // owners
    raw = spectra.reshape(station_count, full_width)
    panel_raw = lax.all_gather(raw, "pairs", axis=0, tiled=True)
    spectrum = raw.astype(jnp.float32)
    local_power = jnp.sum(spectrum * spectrum, axis=1)
    total_power = lax.psum(local_power, "band")
    entries = band_count * lax.axis_size("band") * full_width
    scale = lax.rsqrt(total_power / entries + 1e-05)
    own_spec = lax.reduce_precision(spectrum * scale[:, None], exponent_bits=8, mantissa_bits=7)
    panel_scale = lax.all_gather(scale, "pairs", axis=0, tiled=True)

    owner_flat = jnp.concatenate([pair_owner[:, 0], pair_owner[:, 1]])
    slot_flat = jnp.concatenate([pair_slot[:, 0], pair_slot[:, 1]])
    position = owner_positions(owner_flat, owners)
    part = capacity // 2
    flat_slot = (position // part) * (owners * part) + owner_flat * part + position % part
    request = (
        jnp.full((2 * owners * part,), station_count, jnp.int32)
        .at[flat_slot]
        .set(slot_flat, unique_indices=True)
    )
    wanted = lax.all_to_all(
        request.reshape(2, owners, part), "pairs", split_axis=1, concat_axis=1, tiled=True
    ).reshape(2, owners * part)

    rows0 = pair_owner[:, 0] * station_count + pair_slot[:, 0]
    rows1 = pair_owner[:, 1] * station_count + pair_slot[:, 1]
    near_raw = panel_raw[rows0]
    far_raw = panel_raw[rows1]
    near_scale = panel_scale[rows0][:, None]
    far_scale = panel_scale[rows1][:, None]
    table = lag_basis(half_width, lag_count)
    obs = observed.reshape(pair_count, lag_count)
    contribs = pair_contributions(
        near_raw, far_raw, near_scale, far_scale, obs,
        win_start[:, None], win_end[:, None], table,
    ).reshape(2 * pair_count, full_width)
    station_ids = jnp.arange(station_count, dtype=jnp.int32)[:, None]
    summed = None
    for half in range(2):
        half_slot = jnp.where(position // part == half, flat_slot - half * owners * part, -1)
        half_slot = jnp.where(half_slot < 0, owners * part, half_slot)
        outgoing = (
            jnp.zeros((owners * part, full_width), jnp.bfloat16)
            .at[half_slot]
            .set(contribs, mode="drop")
        )
        incoming = lax.all_to_all(
            outgoing.reshape(owners, part, full_width),
            "pairs",
            split_axis=0,
            concat_axis=0,
            tiled=True,
        ).reshape(owners * part, full_width)
        onehot = (wanted[half][None, :] == station_ids).astype(jnp.bfloat16)
        partial = jnp.dot(onehot, incoming, preferred_element_type=jnp.float32)
        summed = partial if summed is None else summed + partial
    result = 0.25 * (
        summed[:, :half_width] * own_spec[:, :half_width]
        + summed[:, half_width:] * own_spec[:, half_width:]
    )
    return result.reshape(station_count, band_count, half_width)


def solution(mesh):
    return jax.shard_map(
        shards,
        mesh=mesh,
        in_specs=(
            P("pairs", "band", None),
            P("pairs", "band", None),
            P("pairs", None),
            P("pairs", None),
            P("pairs"),
            P("pairs"),
        ),
        out_specs=P("pairs", "band", None),
        check_vma=False,
    )
```

```python
import math

import jax
import jax.numpy as jnp
from jax import lax
from jax.sharding import PartitionSpec as P
from jax.experimental import pallas as pl
from jax.experimental.pallas import tpu as pltpu


def lag_basis(half_width, lag_count):
    freqs = jnp.arange(half_width, dtype=jnp.int32)
    lag_index = jnp.arange(lag_count, dtype=jnp.int32)
    phases = (freqs[:, None] * lag_index[None, :] % lag_count).astype(jnp.float32) * (
        2.0 * math.pi / lag_count
    )
    factor = 1.0 / math.sqrt(lag_count)
    return jnp.concatenate([jnp.cos(phases) * factor, -jnp.sin(phases) * factor], axis=0).astype(
        jnp.bfloat16
    )


def owner_positions(owner_flat, owner_count):
    onehot = (owner_flat[:, None] == jnp.arange(owner_count, dtype=jnp.int32)[None, :]).astype(
        jnp.int32
    )
    before = jnp.cumsum(onehot, axis=0) - onehot
    return jnp.sum(before * onehot, axis=1)


def round_bf16(x):
    return x.astype(jnp.bfloat16).astype(jnp.float32)


def pair_kernel(near_ref, far_ref, ns_ref, fs_ref, obs_ref, ws_ref, we_ref, table_ref, out_ref):
    half = near_ref.shape[1] // 2
    near = round_bf16(near_ref[...].astype(jnp.float32) * ns_ref[...])
    far = round_bf16(far_ref[...].astype(jnp.float32) * fs_ref[...])
    near_re, near_im = near[:, :half], near[:, half:]
    far_re, far_im = far[:, :half], far[:, half:]
    cross_re = (near_re * far_re + near_im * far_im).astype(jnp.bfloat16)
    cross_im = (near_im * far_re - near_re * far_im).astype(jnp.bfloat16)
    tab_re = table_ref[:half, :]
    tab_im = table_ref[half:, :]
    lagged = jnp.dot(cross_re, tab_re, preferred_element_type=jnp.float32) + jnp.dot(
        cross_im, tab_im, preferred_element_type=jnp.float32
    )
    lag = lax.broadcasted_iota(jnp.int32, lagged.shape, 1)
    inside = (lag >= ws_ref[...]) & (lag < we_ref[...])
    residual = jnp.where(inside, lagged - obs_ref[...].astype(jnp.float32), 0.0).astype(
        jnp.bfloat16
    )
    dims = (((1,), (1,)), ((), ()))
    adj_re = lax.dot_general(residual, tab_re, dims, preferred_element_type=jnp.float32)
    adj_im = lax.dot_general(residual, tab_im, dims, preferred_element_type=jnp.float32)
    out_ref[0, :, :half] = (adj_re * far_re - adj_im * far_im).astype(jnp.bfloat16)
    out_ref[0, :, half:] = (adj_re * far_im + adj_im * far_re).astype(jnp.bfloat16)
    out_ref[1, :, :half] = (adj_re * near_re + adj_im * near_im).astype(jnp.bfloat16)
    out_ref[1, :, half:] = (adj_re * near_im - adj_im * near_re).astype(jnp.bfloat16)


def pair_contributions(near_raw, far_raw, near_scale, far_scale, obs, ws, we, table, block=256):
    pairs, width = near_raw.shape
    lags = obs.shape[1]
    row = lambda i: (i, 0)
    return pl.pallas_call(
        pair_kernel,
        grid=(pairs // block,),
        in_specs=[
            pl.BlockSpec((block, width), row),
            pl.BlockSpec((block, width), row),
            pl.BlockSpec((block, 1), row),
            pl.BlockSpec((block, 1), row),
            pl.BlockSpec((block, lags), row),
            pl.BlockSpec((block, 1), row),
            pl.BlockSpec((block, 1), row),
            pl.BlockSpec((width, lags), lambda i: (0, 0)),
        ],
        out_specs=pl.BlockSpec((2, block, width), lambda i: (0, i, 0)),
        out_shape=jax.ShapeDtypeStruct((2, pairs, width), jnp.bfloat16),
        compiler_params=pltpu.CompilerParams(vmem_limit_bytes=48 * 1024 * 1024),
    )(near_raw, far_raw, near_scale, far_scale, obs, ws, we, table)


def shards(spectra, observed, pair_owner, pair_slot, win_start, win_end):
    owners = lax.axis_size("pairs")
    station_count = spectra.shape[0]
    band_count = spectra.shape[1]
    full_width = spectra.shape[2]
    half_width = full_width // 2
    pair_count = observed.shape[0]
    lag_count = observed.shape[2]
    capacity = 3 * pair_count // owners
    raw = spectra.reshape(station_count, full_width)
    panel_raw = lax.all_gather(raw, "pairs", axis=0, tiled=True)
    spectrum = raw.astype(jnp.float32)
    local_power = jnp.sum(spectrum * spectrum, axis=1)
    total_power = lax.psum(local_power, "band")
    entries = band_count * lax.axis_size("band") * full_width
    scale = lax.rsqrt(total_power / entries + 1e-05)
    own_spec = lax.reduce_precision(spectrum * scale[:, None], exponent_bits=8, mantissa_bits=7)
    panel_scale = lax.all_gather(scale, "pairs", axis=0, tiled=True)

    owner_flat = jnp.concatenate([pair_owner[:, 0], pair_owner[:, 1]])
    slot_flat = jnp.concatenate([pair_slot[:, 0], pair_slot[:, 1]])
    position = owner_positions(owner_flat, owners)
    rows0 = pair_owner[:, 0] * station_count + pair_slot[:, 0]
    rows1 = pair_owner[:, 1] * station_count + pair_slot[:, 1]
    near_raw = panel_raw[rows0]
    far_raw = panel_raw[rows1]
    near_scale = panel_scale[rows0][:, None]
    far_scale = panel_scale[rows1][:, None]
    table = lag_basis(half_width, lag_count)
    obs = observed.reshape(pair_count, lag_count)
    contribs = pair_contributions(
        near_raw, far_raw, near_scale, far_scale, obs,
        win_start[:, None], win_end[:, None], table,
    ).reshape(2 * pair_count, full_width)
    endpoint_rows = jnp.concatenate([rows0, rows1])
    dense = (
        jnp.zeros((owners * station_count, full_width), jnp.float32)
        .at[endpoint_rows]
        .add(contribs.astype(jnp.float32))
    ).astype(jnp.bfloat16)
    summed = lax.psum_scatter(dense, "pairs", scatter_dimension=0, tiled=True).astype(
        jnp.float32
    )
    result = 0.25 * (
        summed[:, :half_width] * own_spec[:, :half_width]
        + summed[:, half_width:] * own_spec[:, half_width:]
    )
    return result.reshape(station_count, band_count, half_width)


def solution(mesh):
    return jax.shard_map(
        shards,
        mesh=mesh,
        in_specs=(
            P("pairs", "band", None),
            P("pairs", "band", None),
            P("pairs", None),
            P("pairs", None),
            P("pairs"),
            P("pairs"),
        ),
        out_specs=P("pairs", "band", None),
        check_vma=False,
    )
```

```python
import math

import jax
import jax.numpy as jnp
from jax import lax
from jax.sharding import PartitionSpec as P
from jax.experimental import pallas as pl
from jax.experimental.pallas import tpu as pltpu


def lag_basis(half_width, lag_count):
    freqs = jnp.arange(half_width, dtype=jnp.int32)
    lag_index = jnp.arange(lag_count, dtype=jnp.int32)
    phases = (freqs[:, None] * lag_index[None, :] % lag_count).astype(jnp.float32) * (
        2.0 * math.pi / lag_count
    )
    factor = 1.0 / math.sqrt(lag_count)
    return jnp.concatenate([jnp.cos(phases) * factor, -jnp.sin(phases) * factor], axis=0).astype(
        jnp.bfloat16
    )


def owner_positions(owner_flat, owner_count):
    onehot = (owner_flat[:, None] == jnp.arange(owner_count, dtype=jnp.int32)[None, :]).astype(
        jnp.int32
    )
    before = jnp.cumsum(onehot, axis=0) - onehot
    return jnp.sum(before * onehot, axis=1)


def round_bf16(x):
    return x.astype(jnp.bfloat16).astype(jnp.float32)


def pair_kernel(near_ref, far_ref, ns_ref, fs_ref, obs_ref, ws_ref, we_ref, table_ref, out_ref):
    half = near_ref.shape[1] // 2
    near = round_bf16(near_ref[...].astype(jnp.float32) * ns_ref[...])
    far = round_bf16(far_ref[...].astype(jnp.float32) * fs_ref[...])
    near_re, near_im = near[:, :half], near[:, half:]
    far_re, far_im = far[:, :half], far[:, half:]
    cross_re = (near_re * far_re + near_im * far_im).astype(jnp.bfloat16)
    cross_im = (near_im * far_re - near_re * far_im).astype(jnp.bfloat16)
    tab_re = table_ref[:half, :]
    tab_im = table_ref[half:, :]
    lagged = jnp.dot(cross_re, tab_re, preferred_element_type=jnp.float32) + jnp.dot(
        cross_im, tab_im, preferred_element_type=jnp.float32
    )
    lag = lax.broadcasted_iota(jnp.int32, lagged.shape, 1)
    inside = (lag >= ws_ref[...]) & (lag < we_ref[...])
    residual = jnp.where(inside, lagged - obs_ref[...].astype(jnp.float32), 0.0).astype(
        jnp.bfloat16
    )
    dims = (((1,), (1,)), ((), ()))
    adj_re = lax.dot_general(residual, tab_re, dims, preferred_element_type=jnp.float32)
    adj_im = lax.dot_general(residual, tab_im, dims, preferred_element_type=jnp.float32)
    out_ref[0, :, :half] = (adj_re * far_re - adj_im * far_im).astype(jnp.bfloat16)
    out_ref[0, :, half:] = (adj_re * far_im + adj_im * far_re).astype(jnp.bfloat16)
    out_ref[1, :, :half] = (adj_re * near_re + adj_im * near_im).astype(jnp.bfloat16)
    out_ref[1, :, half:] = (adj_re * near_im - adj_im * near_re).astype(jnp.bfloat16)


def pair_contributions(near_raw, far_raw, near_scale, far_scale, obs, ws, we, table, block=256):
    pairs, width = near_raw.shape
    lags = obs.shape[1]
    row = lambda i: (i, 0)
    return pl.pallas_call(
        pair_kernel,
        grid=(pairs // block,),
        in_specs=[
            pl.BlockSpec((block, width), row),
            pl.BlockSpec((block, width), row),
            pl.BlockSpec((block, 1), row),
            pl.BlockSpec((block, 1), row),
            pl.BlockSpec((block, lags), row),
            pl.BlockSpec((block, 1), row),
            pl.BlockSpec((block, 1), row),
            pl.BlockSpec((width, lags), lambda i: (0, 0)),
        ],
        out_specs=pl.BlockSpec((2, block, width), lambda i: (0, i, 0)),
        out_shape=jax.ShapeDtypeStruct((2, pairs, width), jnp.bfloat16),
        compiler_params=pltpu.CompilerParams(vmem_limit_bytes=48 * 1024 * 1024),
    )(near_raw, far_raw, near_scale, far_scale, obs, ws, we, table)


def shards(spectra, observed, pair_owner, pair_slot, win_start, win_end):
    owners = lax.axis_size("pairs")
    station_count = spectra.shape[0]
    band_count = spectra.shape[1]
    full_width = spectra.shape[2]
    half_width = full_width // 2
    pair_count = observed.shape[0]
    lag_count = observed.shape[2]
    capacity = 3 * pair_count // owners
    raw = spectra.reshape(station_count, full_width)
    panel_raw = lax.all_gather(raw, "pairs", axis=0, tiled=True)
    spectrum = raw.astype(jnp.float32)
    local_power = jnp.sum(spectrum * spectrum, axis=1)
    total_power = lax.psum(local_power, "band")
    entries = band_count * lax.axis_size("band") * full_width
    scale = lax.rsqrt(total_power / entries + 1e-05)
    own_spec = lax.reduce_precision(spectrum * scale[:, None], exponent_bits=8, mantissa_bits=7)
    panel_scale = lax.all_gather(scale, "pairs", axis=0, tiled=True)

    rows0 = pair_owner[:, 0] * station_count + pair_slot[:, 0]
    rows1 = pair_owner[:, 1] * station_count + pair_slot[:, 1]
    near_raw = panel_raw[rows0]
    far_raw = panel_raw[rows1]
    near_scale = panel_scale[rows0][:, None]
    far_scale = panel_scale[rows1][:, None]
    table = lag_basis(half_width, lag_count)
    obs = observed.reshape(pair_count, lag_count)
    contribs = pair_contributions(
        near_raw, far_raw, near_scale, far_scale, obs,
        win_start[:, None], win_end[:, None], table,
    ).reshape(2 * pair_count, full_width)
    endpoint_rows = jnp.concatenate([rows0, rows1])
    dense = (
        jnp.zeros((owners * station_count, full_width), jnp.bfloat16)
        .at[endpoint_rows]
        .add(contribs)
    )
    summed = lax.psum_scatter(dense, "pairs", scatter_dimension=0, tiled=True).astype(
        jnp.float32
    )
    result = 0.25 * (
        summed[:, :half_width] * own_spec[:, :half_width]
        + summed[:, half_width:] * own_spec[:, half_width:]
    )
    return result.reshape(station_count, band_count, half_width)


def solution(mesh):
    return jax.shard_map(
        shards,
        mesh=mesh,
        in_specs=(
            P("pairs", "band", None),
            P("pairs", "band", None),
            P("pairs", None),
            P("pairs", None),
            P("pairs"),
            P("pairs"),
        ),
        out_specs=P("pairs", "band", None),
        check_vma=False,
    )
```

```python
import math

import jax
import jax.numpy as jnp
from jax import lax
from jax.sharding import PartitionSpec as P
from jax.experimental import pallas as pl
from jax.experimental.pallas import tpu as pltpu


def lag_basis(half_width, lag_count):
    freqs = jnp.arange(half_width, dtype=jnp.int32)
    lag_index = jnp.arange(lag_count, dtype=jnp.int32)
    phases = (freqs[:, None] * lag_index[None, :] % lag_count).astype(jnp.float32) * (
        2.0 * math.pi / lag_count
    )
    factor = 1.0 / math.sqrt(lag_count)
    return jnp.concatenate([jnp.cos(phases) * factor, -jnp.sin(phases) * factor], axis=0).astype(
        jnp.bfloat16
    )


def owner_positions(owner_flat, owner_count):
    onehot = (owner_flat[:, None] == jnp.arange(owner_count, dtype=jnp.int32)[None, :]).astype(
        jnp.int32
    )
    before = jnp.cumsum(onehot, axis=0) - onehot
    return jnp.sum(before * onehot, axis=1)


def round_bf16(x):
    return x.astype(jnp.bfloat16).astype(jnp.float32)


def pair_kernel(near_ref, far_ref, ns_ref, fs_ref, obs_ref, ws_ref, we_ref, table_ref, out_ref):
    half = near_ref.shape[1] // 2
    near = round_bf16(near_ref[...].astype(jnp.float32) * ns_ref[...])
    far = round_bf16(far_ref[...].astype(jnp.float32) * fs_ref[...])
    near_re, near_im = near[:, :half], near[:, half:]
    far_re, far_im = far[:, :half], far[:, half:]
    cross_re = (near_re * far_re + near_im * far_im).astype(jnp.bfloat16)
    cross_im = (near_im * far_re - near_re * far_im).astype(jnp.bfloat16)
    tab_re = table_ref[:half, :]
    tab_im = table_ref[half:, :]
    lagged = jnp.dot(cross_re, tab_re, preferred_element_type=jnp.float32) + jnp.dot(
        cross_im, tab_im, preferred_element_type=jnp.float32
    )
    lag = lax.broadcasted_iota(jnp.int32, lagged.shape, 1)
    inside = (lag >= ws_ref[...]) & (lag < we_ref[...])
    residual = jnp.where(inside, lagged - obs_ref[...].astype(jnp.float32), 0.0).astype(
        jnp.bfloat16
    )
    dims = (((1,), (1,)), ((), ()))
    adj_re = lax.dot_general(residual, tab_re, dims, preferred_element_type=jnp.float32)
    adj_im = lax.dot_general(residual, tab_im, dims, preferred_element_type=jnp.float32)
    out_ref[0, :, :half] = (adj_re * far_re - adj_im * far_im).astype(jnp.bfloat16)
    out_ref[0, :, half:] = (adj_re * far_im + adj_im * far_re).astype(jnp.bfloat16)
    out_ref[1, :, :half] = (adj_re * near_re + adj_im * near_im).astype(jnp.bfloat16)
    out_ref[1, :, half:] = (adj_re * near_im - adj_im * near_re).astype(jnp.bfloat16)


def pair_contributions(near_raw, far_raw, near_scale, far_scale, obs, ws, we, table, block=256):
    pairs, width = near_raw.shape
    lags = obs.shape[1]
    row = lambda i: (i, 0)
    return pl.pallas_call(
        pair_kernel,
        grid=(pairs // block,),
        in_specs=[
            pl.BlockSpec((block, width), row),
            pl.BlockSpec((block, width), row),
            pl.BlockSpec((block, 1), row),
            pl.BlockSpec((block, 1), row),
            pl.BlockSpec((block, lags), row),
            pl.BlockSpec((block, 1), row),
            pl.BlockSpec((block, 1), row),
            pl.BlockSpec((width, lags), lambda i: (0, 0)),
        ],
        out_specs=pl.BlockSpec((2, block, width), lambda i: (0, i, 0)),
        out_shape=jax.ShapeDtypeStruct((2, pairs, width), jnp.bfloat16),
        compiler_params=pltpu.CompilerParams(vmem_limit_bytes=48 * 1024 * 1024),
    )(near_raw, far_raw, near_scale, far_scale, obs, ws, we, table)


def shards(spectra, observed, pair_owner, pair_slot, win_start, win_end):
    owners = lax.axis_size("pairs")
    station_count = spectra.shape[0]
    band_count = spectra.shape[1]
    full_width = spectra.shape[2]
    half_width = full_width // 2
    pair_count = observed.shape[0]
    lag_count = observed.shape[2]
    capacity = 3 * pair_count // owners
    raw = spectra.reshape(station_count, full_width)
    panel_raw = lax.all_gather(raw, "pairs", axis=0, tiled=True)
    spectrum = raw.astype(jnp.float32)
    local_power = jnp.sum(spectrum * spectrum, axis=1)
    total_power = lax.psum(local_power, "band")
    entries = band_count * lax.axis_size("band") * full_width
    scale = lax.rsqrt(total_power / entries + 1e-05)
    own_spec = lax.reduce_precision(spectrum * scale[:, None], exponent_bits=8, mantissa_bits=7)
    panel_scale = lax.all_gather(scale, "pairs", axis=0, tiled=True)

    rows0 = pair_owner[:, 0] * station_count + pair_slot[:, 0]
    rows1 = pair_owner[:, 1] * station_count + pair_slot[:, 1]
    near_raw = panel_raw[rows0]
    far_raw = panel_raw[rows1]
    near_scale = panel_scale[rows0][:, None]
    far_scale = panel_scale[rows1][:, None]
    table = lag_basis(half_width, lag_count)
    obs = observed.reshape(pair_count, lag_count)
    contribs = pair_contributions(
        near_raw, far_raw, near_scale, far_scale, obs,
        win_start[:, None], win_end[:, None], table,
    ).reshape(2 * pair_count, full_width)
    owner_flat = jnp.concatenate([pair_owner[:, 0], pair_owner[:, 1]])
    slot_flat = jnp.concatenate([pair_slot[:, 0], pair_slot[:, 1]])
    position = owner_positions(owner_flat, owners)
    flat_slot = owner_flat * capacity + position
    slot_station = (
        jnp.full((owners * capacity,), station_count, jnp.int32)
        .at[flat_slot]
        .set(slot_flat, unique_indices=True)
    ).reshape(owners, 1, capacity)
    slotted = (
        jnp.zeros((owners * capacity, full_width), jnp.bfloat16)
        .at[flat_slot]
        .set(contribs, unique_indices=True)
    ).reshape(owners, capacity, full_width)
    station_ids = jnp.arange(station_count, dtype=jnp.int32)[None, :, None]
    onehot = (slot_station == station_ids).astype(jnp.bfloat16)
    dense = jnp.einsum(
        "osk,okf->osf", onehot, slotted, preferred_element_type=jnp.float32
    ).astype(jnp.bfloat16).reshape(owners * station_count, full_width)
    summed = lax.psum_scatter(dense, "pairs", scatter_dimension=0, tiled=True).astype(
        jnp.float32
    )
    result = 0.25 * (
        summed[:, :half_width] * own_spec[:, :half_width]
        + summed[:, half_width:] * own_spec[:, half_width:]
    )
    return result.reshape(station_count, band_count, half_width)


def solution(mesh):
    return jax.shard_map(
        shards,
        mesh=mesh,
        in_specs=(
            P("pairs", "band", None),
            P("pairs", "band", None),
            P("pairs", None),
            P("pairs", None),
            P("pairs"),
            P("pairs"),
        ),
        out_specs=P("pairs", "band", None),
        check_vma=False,
    )
```

```python
import math

import jax
import jax.numpy as jnp
from jax import lax
from jax.sharding import PartitionSpec as P
from jax.experimental import pallas as pl
from jax.experimental.pallas import tpu as pltpu


def lag_basis(half_width, lag_count):
    freqs = jnp.arange(half_width, dtype=jnp.int32)
    lag_index = jnp.arange(lag_count, dtype=jnp.int32)
    phases = (freqs[:, None] * lag_index[None, :] % lag_count).astype(jnp.float32) * (
        2.0 * math.pi / lag_count
    )
    factor = 1.0 / math.sqrt(lag_count)
    return jnp.concatenate([jnp.cos(phases) * factor, -jnp.sin(phases) * factor], axis=0).astype(
        jnp.bfloat16
    )


def owner_positions(owner_flat, owner_count):
    onehot = (owner_flat[:, None] == jnp.arange(owner_count, dtype=jnp.int32)[None, :]).astype(
        jnp.int32
    )
    before = jnp.cumsum(onehot, axis=0) - onehot
    return jnp.sum(before * onehot, axis=1)


def round_bf16(x):
    return x.astype(jnp.bfloat16).astype(jnp.float32)


def pair_kernel(near_ref, far_ref, ns_ref, fs_ref, obs_ref, ws_ref, we_ref, table_ref, out_ref):
    half = near_ref.shape[1] // 2
    near = round_bf16(near_ref[...].astype(jnp.float32) * ns_ref[...])
    far = round_bf16(far_ref[...].astype(jnp.float32) * fs_ref[...])
    near_re, near_im = near[:, :half], near[:, half:]
    far_re, far_im = far[:, :half], far[:, half:]
    cross_re = (near_re * far_re + near_im * far_im).astype(jnp.bfloat16)
    cross_im = (near_im * far_re - near_re * far_im).astype(jnp.bfloat16)
    tab_re = table_ref[:half, :]
    tab_im = table_ref[half:, :]
    lagged = jnp.dot(cross_re, tab_re, preferred_element_type=jnp.float32) + jnp.dot(
        cross_im, tab_im, preferred_element_type=jnp.float32
    )
    lag = lax.broadcasted_iota(jnp.int32, lagged.shape, 1)
    inside = (lag >= ws_ref[...]) & (lag < we_ref[...])
    residual = jnp.where(inside, lagged - obs_ref[...].astype(jnp.float32), 0.0).astype(
        jnp.bfloat16
    )
    dims = (((1,), (1,)), ((), ()))
    adj_re = lax.dot_general(residual, tab_re, dims, preferred_element_type=jnp.float32)
    adj_im = lax.dot_general(residual, tab_im, dims, preferred_element_type=jnp.float32)
    out_ref[0, :, :half] = (adj_re * far_re - adj_im * far_im).astype(jnp.bfloat16)
    out_ref[0, :, half:] = (adj_re * far_im + adj_im * far_re).astype(jnp.bfloat16)
    out_ref[1, :, :half] = (adj_re * near_re + adj_im * near_im).astype(jnp.bfloat16)
    out_ref[1, :, half:] = (adj_re * near_im - adj_im * near_re).astype(jnp.bfloat16)


def pair_contributions(near_raw, far_raw, near_scale, far_scale, obs, ws, we, table, block=256):
    pairs, width = near_raw.shape
    lags = obs.shape[1]
    row = lambda i: (i, 0)
    return pl.pallas_call(
        pair_kernel,
        grid=(pairs // block,),
        in_specs=[
            pl.BlockSpec((block, width), row),
            pl.BlockSpec((block, width), row),
            pl.BlockSpec((block, 1), row),
            pl.BlockSpec((block, 1), row),
            pl.BlockSpec((block, lags), row),
            pl.BlockSpec((block, 1), row),
            pl.BlockSpec((block, 1), row),
            pl.BlockSpec((width, lags), lambda i: (0, 0)),
        ],
        out_specs=pl.BlockSpec((2, block, width), lambda i: (0, i, 0)),
        out_shape=jax.ShapeDtypeStruct((2, pairs, width), jnp.bfloat16),
        compiler_params=pltpu.CompilerParams(vmem_limit_bytes=48 * 1024 * 1024),
    )(near_raw, far_raw, near_scale, far_scale, obs, ws, we, table)


def shards(spectra, observed, pair_owner, pair_slot, win_start, win_end):
    owners = lax.axis_size("pairs")
    station_count = spectra.shape[0]
    band_count = spectra.shape[1]
    full_width = spectra.shape[2]
    half_width = full_width // 2
    pair_count = observed.shape[0]
    lag_count = observed.shape[2]
    capacity = 3 * pair_count // owners
    raw = spectra.reshape(station_count, full_width)
    panel_raw = lax.all_gather(raw, "pairs", axis=0, tiled=True)
    spectrum = raw.astype(jnp.float32)
    local_power = jnp.sum(spectrum * spectrum, axis=1)
    total_power = lax.psum(local_power, "band")
    entries = band_count * lax.axis_size("band") * full_width
    scale = lax.rsqrt(total_power / entries + 1e-05)
    own_spec = lax.reduce_precision(spectrum * scale[:, None], exponent_bits=8, mantissa_bits=7)
    panel_scale = lax.all_gather(scale, "pairs", axis=0, tiled=True)

    rows0 = pair_owner[:, 0] * station_count + pair_slot[:, 0]
    rows1 = pair_owner[:, 1] * station_count + pair_slot[:, 1]
    near_raw = panel_raw[rows0]
    far_raw = panel_raw[rows1]
    near_scale = panel_scale[rows0][:, None]
    far_scale = panel_scale[rows1][:, None]
    table = lag_basis(half_width, lag_count)
    obs = observed.reshape(pair_count, lag_count)
    contribs = pair_contributions(
        near_raw, far_raw, near_scale, far_scale, obs,
        win_start[:, None], win_end[:, None], table,
    ).reshape(2 * pair_count, full_width)
    owner_flat = jnp.concatenate([pair_owner[:, 0], pair_owner[:, 1]])
    slot_flat = jnp.concatenate([pair_slot[:, 0], pair_slot[:, 1]])
    position = owner_positions(owner_flat, owners)
    flat_slot = owner_flat * capacity + position
    slot_station = (
        jnp.full((owners * capacity,), station_count, jnp.int32)
        .at[flat_slot]
        .set(slot_flat, unique_indices=True)
    ).reshape(owners, 1, capacity)
    slotted = (
        jnp.zeros((owners * capacity, full_width), jnp.bfloat16)
        .at[flat_slot]
        .set(contribs, unique_indices=True)
    ).reshape(owners, capacity, full_width)
    part = station_count // 2
    summed = []
    for half in range(2):
        station_ids = half * part + jnp.arange(part, dtype=jnp.int32)[None, :, None]
        onehot = (slot_station == station_ids).astype(jnp.bfloat16)
        dense = jnp.einsum(
            "osk,okf->osf", onehot, slotted, preferred_element_type=jnp.float32
        ).astype(jnp.bfloat16).reshape(owners * part, full_width)
        summed.append(lax.psum_scatter(dense, "pairs", scatter_dimension=0, tiled=True))
    summed = jnp.concatenate(summed, axis=0).astype(jnp.float32)
    result = 0.25 * (
        summed[:, :half_width] * own_spec[:, :half_width]
        + summed[:, half_width:] * own_spec[:, half_width:]
    )
    return result.reshape(station_count, band_count, half_width)


def solution(mesh):
    return jax.shard_map(
        shards,
        mesh=mesh,
        in_specs=(
            P("pairs", "band", None),
            P("pairs", "band", None),
            P("pairs", None),
            P("pairs", None),
            P("pairs"),
            P("pairs"),
        ),
        out_specs=P("pairs", "band", None),
        check_vma=False,
    )
```

```python
import math

import jax
import jax.numpy as jnp
from jax import lax
from jax.sharding import PartitionSpec as P
from jax.experimental import pallas as pl
from jax.experimental.pallas import tpu as pltpu


def lag_basis(half_width, lag_count):
    freqs = jnp.arange(half_width, dtype=jnp.int32)
    lag_index = jnp.arange(lag_count, dtype=jnp.int32)
    phases = (freqs[:, None] * lag_index[None, :] % lag_count).astype(jnp.float32) * (
        2.0 * math.pi / lag_count
    )
    factor = 1.0 / math.sqrt(lag_count)
    return jnp.concatenate([jnp.cos(phases) * factor, -jnp.sin(phases) * factor], axis=0).astype(
        jnp.bfloat16
    )


def owner_positions(owner_flat, owner_count):
    onehot = (owner_flat[:, None] == jnp.arange(owner_count, dtype=jnp.int32)[None, :]).astype(
        jnp.int32
    )
    before = jnp.cumsum(onehot, axis=0) - onehot
    return jnp.sum(before * onehot, axis=1)


def round_bf16(x):
    return x.astype(jnp.bfloat16).astype(jnp.float32)


def pair_kernel(near_ref, far_ref, ns_ref, fs_ref, obs_ref, ws_ref, we_ref, table_ref, out_ref):
    half = near_ref.shape[1] // 2
    near = round_bf16(near_ref[...].astype(jnp.float32) * ns_ref[...])
    far = round_bf16(far_ref[...].astype(jnp.float32) * fs_ref[...])
    near_re, near_im = near[:, :half], near[:, half:]
    far_re, far_im = far[:, :half], far[:, half:]
    cross_re = (near_re * far_re + near_im * far_im).astype(jnp.bfloat16)
    cross_im = (near_im * far_re - near_re * far_im).astype(jnp.bfloat16)
    tab_re = table_ref[:half, :]
    tab_im = table_ref[half:, :]
    lagged = jnp.dot(cross_re, tab_re, preferred_element_type=jnp.float32) + jnp.dot(
        cross_im, tab_im, preferred_element_type=jnp.float32
    )
    lag = lax.broadcasted_iota(jnp.int32, lagged.shape, 1)
    inside = (lag >= ws_ref[...]) & (lag < we_ref[...])
    residual = jnp.where(inside, lagged - obs_ref[...].astype(jnp.float32), 0.0).astype(
        jnp.bfloat16
    )
    dims = (((1,), (1,)), ((), ()))
    adj_re = lax.dot_general(residual, tab_re, dims, preferred_element_type=jnp.float32)
    adj_im = lax.dot_general(residual, tab_im, dims, preferred_element_type=jnp.float32)
    out_ref[0, :, :half] = (adj_re * far_re - adj_im * far_im).astype(jnp.bfloat16)
    out_ref[0, :, half:] = (adj_re * far_im + adj_im * far_re).astype(jnp.bfloat16)
    out_ref[1, :, :half] = (adj_re * near_re + adj_im * near_im).astype(jnp.bfloat16)
    out_ref[1, :, half:] = (adj_re * near_im - adj_im * near_re).astype(jnp.bfloat16)


def pair_contributions(near_raw, far_raw, near_scale, far_scale, obs, ws, we, table, block=512):
    pairs, width = near_raw.shape
    lags = obs.shape[1]
    row = lambda i: (i, 0)
    return pl.pallas_call(
        pair_kernel,
        grid=(pairs // block,),
        in_specs=[
            pl.BlockSpec((block, width), row),
            pl.BlockSpec((block, width), row),
            pl.BlockSpec((block, 1), row),
            pl.BlockSpec((block, 1), row),
            pl.BlockSpec((block, lags), row),
            pl.BlockSpec((block, 1), row),
            pl.BlockSpec((block, 1), row),
            pl.BlockSpec((width, lags), lambda i: (0, 0)),
        ],
        out_specs=pl.BlockSpec((2, block, width), lambda i: (0, i, 0)),
        out_shape=jax.ShapeDtypeStruct((2, pairs, width), jnp.bfloat16),
        compiler_params=pltpu.CompilerParams(vmem_limit_bytes=48 * 1024 * 1024),
    )(near_raw, far_raw, near_scale, far_scale, obs, ws, we, table)


def shards(spectra, observed, pair_owner, pair_slot, win_start, win_end):
    owners = lax.axis_size("pairs")
    station_count = spectra.shape[0]
    band_count = spectra.shape[1]
    full_width = spectra.shape[2]
    half_width = full_width // 2
    pair_count = observed.shape[0]
    lag_count = observed.shape[2]
    capacity = 3 * pair_count // owners
    raw = spectra.reshape(station_count, full_width)
    panel_raw = lax.all_gather(raw, "pairs", axis=0, tiled=True)
    spectrum = raw.astype(jnp.float32)
    local_power = jnp.sum(spectrum * spectrum, axis=1)
    total_power = lax.psum(local_power, "band")
    entries = band_count * lax.axis_size("band") * full_width
    scale = lax.rsqrt(total_power / entries + 1e-05)
    own_spec = lax.reduce_precision(spectrum * scale[:, None], exponent_bits=8, mantissa_bits=7)
    panel_scale = lax.all_gather(scale, "pairs", axis=0, tiled=True)

    rows0 = pair_owner[:, 0] * station_count + pair_slot[:, 0]
    rows1 = pair_owner[:, 1] * station_count + pair_slot[:, 1]
    near_raw = panel_raw[rows0]
    far_raw = panel_raw[rows1]
    near_scale = panel_scale[rows0][:, None]
    far_scale = panel_scale[rows1][:, None]
    table = lag_basis(half_width, lag_count)
    obs = observed.reshape(pair_count, lag_count)
    contribs = pair_contributions(
        near_raw, far_raw, near_scale, far_scale, obs,
        win_start[:, None], win_end[:, None], table,
    ).reshape(2 * pair_count, full_width)
    owner_flat = jnp.concatenate([pair_owner[:, 0], pair_owner[:, 1]])
    slot_flat = jnp.concatenate([pair_slot[:, 0], pair_slot[:, 1]])
    position = owner_positions(owner_flat, owners)
    flat_slot = owner_flat * capacity + position
    slot_station = (
        jnp.full((owners * capacity,), station_count, jnp.int32)
        .at[flat_slot]
        .set(slot_flat, unique_indices=True)
    ).reshape(owners, 1, capacity)
    slotted = (
        jnp.zeros((owners * capacity, full_width), jnp.bfloat16)
        .at[flat_slot]
        .set(contribs, unique_indices=True)
    ).reshape(owners, capacity, full_width)
    station_ids = jnp.arange(station_count, dtype=jnp.int32)[None, :, None]
    onehot = (slot_station == station_ids).astype(jnp.bfloat16)
    dense = jnp.einsum(
        "osk,okf->osf", onehot, slotted, preferred_element_type=jnp.float32
    ).astype(jnp.bfloat16).reshape(owners * station_count, full_width)
    summed = lax.psum_scatter(dense, "pairs", scatter_dimension=0, tiled=True).astype(
        jnp.float32
    )
    result = 0.25 * (
        summed[:, :half_width] * own_spec[:, :half_width]
        + summed[:, half_width:] * own_spec[:, half_width:]
    )
    return result.reshape(station_count, band_count, half_width)


def solution(mesh):
    return jax.shard_map(
        shards,
        mesh=mesh,
        in_specs=(
            P("pairs", "band", None),
            P("pairs", "band", None),
            P("pairs", None),
            P("pairs", None),
            P("pairs"),
            P("pairs"),
        ),
        out_specs=P("pairs", "band", None),
        check_vma=False,
    )
```

```python
import math

import jax
import jax.numpy as jnp
from jax import lax
from jax.sharding import PartitionSpec as P
from jax.experimental import pallas as pl
from jax.experimental.pallas import tpu as pltpu


def lag_basis(half_width, lag_count):
    freqs = jnp.arange(half_width, dtype=jnp.int32)
    lag_index = jnp.arange(lag_count, dtype=jnp.int32)
    phases = (freqs[:, None] * lag_index[None, :] % lag_count).astype(jnp.float32) * (
        2.0 * math.pi / lag_count
    )
    factor = 1.0 / math.sqrt(lag_count)
    return jnp.concatenate([jnp.cos(phases) * factor, -jnp.sin(phases) * factor], axis=0).astype(
        jnp.bfloat16
    )


def owner_positions(owner_flat, owner_count):
    onehot = (owner_flat[:, None] == jnp.arange(owner_count, dtype=jnp.int32)[None, :]).astype(
        jnp.int32
    )
    before = jnp.cumsum(onehot, axis=0) - onehot
    return jnp.sum(before * onehot, axis=1)


def round_bf16(x):
    return x.astype(jnp.bfloat16).astype(jnp.float32)


def pair_kernel(near_ref, far_ref, ns_ref, fs_ref, obs_ref, ws_ref, we_ref, table_ref, out_ref):
    half = near_ref.shape[1] // 2
    near = round_bf16(near_ref[...].astype(jnp.float32) * ns_ref[...])
    far = round_bf16(far_ref[...].astype(jnp.float32) * fs_ref[...])
    near_re, near_im = near[:, :half], near[:, half:]
    far_re, far_im = far[:, :half], far[:, half:]
    cross_re = (near_re * far_re + near_im * far_im).astype(jnp.bfloat16)
    cross_im = (near_im * far_re - near_re * far_im).astype(jnp.bfloat16)
    tab_re = table_ref[:half, :]
    tab_im = table_ref[half:, :]
    lagged = jnp.dot(cross_re, tab_re, preferred_element_type=jnp.float32) + jnp.dot(
        cross_im, tab_im, preferred_element_type=jnp.float32
    )
    lag = lax.broadcasted_iota(jnp.int32, lagged.shape, 1)
    inside = (lag >= ws_ref[...]) & (lag < we_ref[...])
    residual = jnp.where(inside, lagged - obs_ref[...].astype(jnp.float32), 0.0).astype(
        jnp.bfloat16
    )
    dims = (((1,), (1,)), ((), ()))
    adj_re = lax.dot_general(residual, tab_re, dims, preferred_element_type=jnp.float32)
    adj_im = lax.dot_general(residual, tab_im, dims, preferred_element_type=jnp.float32)
    out_ref[0, :, :half] = (adj_re * far_re - adj_im * far_im).astype(jnp.bfloat16)
    out_ref[0, :, half:] = (adj_re * far_im + adj_im * far_re).astype(jnp.bfloat16)
    out_ref[1, :, :half] = (adj_re * near_re + adj_im * near_im).astype(jnp.bfloat16)
    out_ref[1, :, half:] = (adj_re * near_im - adj_im * near_re).astype(jnp.bfloat16)


def pair_contributions(near_raw, far_raw, near_scale, far_scale, obs, ws, we, table, block=512):
    pairs, width = near_raw.shape
    lags = obs.shape[1]
    row = lambda i: (i, 0)
    return pl.pallas_call(
        pair_kernel,
        grid=(pairs // block,),
        in_specs=[
            pl.BlockSpec((block, width), row),
            pl.BlockSpec((block, width), row),
            pl.BlockSpec((block, 1), row),
            pl.BlockSpec((block, 1), row),
            pl.BlockSpec((block, lags), row),
            pl.BlockSpec((block, 1), row),
            pl.BlockSpec((block, 1), row),
            pl.BlockSpec((width, lags), lambda i: (0, 0)),
        ],
        out_specs=pl.BlockSpec((2, block, width), lambda i: (0, i, 0)),
        out_shape=jax.ShapeDtypeStruct((2, pairs, width), jnp.bfloat16),
        compiler_params=pltpu.CompilerParams(vmem_limit_bytes=48 * 1024 * 1024),
    )(near_raw, far_raw, near_scale, far_scale, obs, ws, we, table)


def finish_kernel(summed_ref, own_ref, out_ref):
    half = own_ref.shape[1] // 2
    summed = summed_ref[...].astype(jnp.float32)
    own = own_ref[...]
    value = 0.25 * (summed[:, :half] * own[:, :half] + summed[:, half:] * own[:, half:])
    out_ref[...] = value.reshape(out_ref.shape)


def finish(summed, own_spec, band_count):
    stations, width = own_spec.shape
    return pl.pallas_call(
        finish_kernel,
        out_shape=jax.ShapeDtypeStruct((stations, band_count, width // 2), jnp.float32),
    )(summed, own_spec)


def shards(spectra, observed, pair_owner, pair_slot, win_start, win_end):
    owners = lax.axis_size("pairs")
    station_count = spectra.shape[0]
    band_count = spectra.shape[1]
    full_width = spectra.shape[2]
    half_width = full_width // 2
    pair_count = observed.shape[0]
    lag_count = observed.shape[2]
    capacity = 3 * pair_count // owners
    raw = spectra.reshape(station_count, full_width)
    panel_raw = lax.all_gather(raw, "pairs", axis=0, tiled=True)
    spectrum = raw.astype(jnp.float32)
    local_power = jnp.sum(spectrum * spectrum, axis=1)
    total_power = lax.psum(local_power, "band")
    entries = band_count * lax.axis_size("band") * full_width
    scale = lax.rsqrt(total_power / entries + 1e-05)
    own_spec = lax.reduce_precision(spectrum * scale[:, None], exponent_bits=8, mantissa_bits=7)
    panel_scale = lax.all_gather(scale, "pairs", axis=0, tiled=True)

    rows0 = pair_owner[:, 0] * station_count + pair_slot[:, 0]
    rows1 = pair_owner[:, 1] * station_count + pair_slot[:, 1]
    near_raw = panel_raw[rows0]
    far_raw = panel_raw[rows1]
    near_scale = panel_scale[rows0][:, None]
    far_scale = panel_scale[rows1][:, None]
    table = lag_basis(half_width, lag_count)
    obs = observed.reshape(pair_count, lag_count)
    contribs = pair_contributions(
        near_raw, far_raw, near_scale, far_scale, obs,
        win_start[:, None], win_end[:, None], table,
    ).reshape(2 * pair_count, full_width)
    owner_flat = jnp.concatenate([pair_owner[:, 0], pair_owner[:, 1]])
    slot_flat = jnp.concatenate([pair_slot[:, 0], pair_slot[:, 1]])
    position = owner_positions(owner_flat, owners)
    flat_slot = owner_flat * capacity + position
    slot_station = (
        jnp.full((owners * capacity,), station_count, jnp.int32)
        .at[flat_slot]
        .set(slot_flat, unique_indices=True)
    ).reshape(owners, 1, capacity)
    slotted = (
        jnp.zeros((owners * capacity, full_width), jnp.bfloat16)
        .at[flat_slot]
        .set(contribs, unique_indices=True)
    ).reshape(owners, capacity, full_width)
    station_ids = jnp.arange(station_count, dtype=jnp.int32)[None, :, None]
    onehot = (slot_station == station_ids).astype(jnp.bfloat16)
    dense = jnp.einsum(
        "osk,okf->osf", onehot, slotted, preferred_element_type=jnp.float32
    ).astype(jnp.bfloat16).reshape(owners * station_count, full_width)
    summed = lax.psum_scatter(dense, "pairs", scatter_dimension=0, tiled=True)
    return finish(summed, own_spec, band_count)


def solution(mesh):
    return jax.shard_map(
        shards,
        mesh=mesh,
        in_specs=(
            P("pairs", "band", None),
            P("pairs", "band", None),
            P("pairs", None),
            P("pairs", None),
            P("pairs"),
            P("pairs"),
        ),
        out_specs=P("pairs", "band", None),
        check_vma=False,
    )
```

```python
import math

import jax
import jax.numpy as jnp
from jax import lax
from jax.sharding import PartitionSpec as P
from jax.experimental import pallas as pl
from jax.experimental.pallas import tpu as pltpu


def lag_basis(half_width, lag_count):
    freqs = jnp.arange(half_width, dtype=jnp.int32)
    lag_index = jnp.arange(lag_count, dtype=jnp.int32)
    phases = (freqs[:, None] * lag_index[None, :] % lag_count).astype(jnp.float32) * (
        2.0 * math.pi / lag_count
    )
    factor = 1.0 / math.sqrt(lag_count)
    return jnp.concatenate([jnp.cos(phases) * factor, -jnp.sin(phases) * factor], axis=0).astype(
        jnp.bfloat16
    )


def owner_positions(owner_flat, owner_count):
    onehot = (owner_flat[:, None] == jnp.arange(owner_count, dtype=jnp.int32)[None, :]).astype(
        jnp.int32
    )
    before = jnp.cumsum(onehot, axis=0) - onehot
    return jnp.sum(before * onehot, axis=1)


def round_bf16(x):
    return x.astype(jnp.bfloat16).astype(jnp.float32)


def pair_kernel(near_ref, far_ref, ns_ref, fs_ref, obs_ref, ws_ref, we_ref, table_ref, out_ref):
    half = near_ref.shape[1] // 2
    near = round_bf16(near_ref[...].astype(jnp.float32) * ns_ref[...])
    far = round_bf16(far_ref[...].astype(jnp.float32) * fs_ref[...])
    near_re, near_im = near[:, :half], near[:, half:]
    far_re, far_im = far[:, :half], far[:, half:]
    cross_re = (near_re * far_re + near_im * far_im).astype(jnp.bfloat16)
    cross_im = (near_im * far_re - near_re * far_im).astype(jnp.bfloat16)
    tab_re = table_ref[:half, :]
    tab_im = table_ref[half:, :]
    lagged = jnp.dot(cross_re, tab_re, preferred_element_type=jnp.float32) + jnp.dot(
        cross_im, tab_im, preferred_element_type=jnp.float32
    )
    lag = lax.broadcasted_iota(jnp.int32, lagged.shape, 1)
    inside = (lag >= ws_ref[...]) & (lag < we_ref[...])
    residual = jnp.where(inside, lagged - obs_ref[...].astype(jnp.float32), 0.0).astype(
        jnp.bfloat16
    )
    dims = (((1,), (1,)), ((), ()))
    adj_re = lax.dot_general(residual, tab_re, dims, preferred_element_type=jnp.float32)
    adj_im = lax.dot_general(residual, tab_im, dims, preferred_element_type=jnp.float32)
    out_ref[0, :, :half] = (adj_re * far_re - adj_im * far_im).astype(jnp.bfloat16)
    out_ref[0, :, half:] = (adj_re * far_im + adj_im * far_re).astype(jnp.bfloat16)
    out_ref[1, :, :half] = (adj_re * near_re + adj_im * near_im).astype(jnp.bfloat16)
    out_ref[1, :, half:] = (adj_re * near_im - adj_im * near_re).astype(jnp.bfloat16)


def pair_contributions(near_raw, far_raw, near_scale, far_scale, obs, ws, we, table, block=512):
    pairs, width = near_raw.shape
    lags = obs.shape[1]
    row = lambda i: (i, 0)
    return pl.pallas_call(
        pair_kernel,
        grid=(pairs // block,),
        in_specs=[
            pl.BlockSpec((block, width), row),
            pl.BlockSpec((block, width), row),
            pl.BlockSpec((block, 1), row),
            pl.BlockSpec((block, 1), row),
            pl.BlockSpec((block, lags), row),
            pl.BlockSpec((block, 1), row),
            pl.BlockSpec((block, 1), row),
            pl.BlockSpec((width, lags), lambda i: (0, 0)),
        ],
        out_specs=pl.BlockSpec((2, block, width), lambda i: (0, i, 0)),
        out_shape=jax.ShapeDtypeStruct((2, pairs, width), jnp.bfloat16),
        compiler_params=pltpu.CompilerParams(vmem_limit_bytes=48 * 1024 * 1024),
    )(near_raw, far_raw, near_scale, far_scale, obs, ws, we, table)


def finish_kernel(summed_ref, own_ref, out_ref):
    half = own_ref.shape[1] // 2
    summed = summed_ref[...].astype(jnp.float32)
    own = own_ref[...]
    value = 0.25 * (summed[:, :half] * own[:, :half] + summed[:, half:] * own[:, half:])
    out_ref[...] = value.reshape(out_ref.shape)


def finish(summed, own_spec, band_count):
    stations, width = own_spec.shape
    return pl.pallas_call(
        finish_kernel,
        out_shape=jax.ShapeDtypeStruct((stations, band_count, width // 2), jnp.float32),
    )(summed, own_spec)


def shards(spectra, observed, pair_owner, pair_slot, win_start, win_end):
    owners = lax.axis_size(("z_hi", "x", "core"))
    station_count = spectra.shape[0]
    band_count = spectra.shape[1]
    full_width = spectra.shape[2]
    half_width = full_width // 2
    pair_count = observed.shape[0]
    lag_count = observed.shape[2]
    capacity = 3 * pair_count // owners
    raw = spectra.reshape(station_count, full_width)
    panel_raw = lax.all_gather(raw, ("z_hi", "x", "core"), axis=0, tiled=True)
    spectrum = raw.astype(jnp.float32)
    local_power = jnp.sum(spectrum * spectrum, axis=1)
    total_power = lax.psum(local_power, ("y", "z_lo"))
    entries = band_count * lax.axis_size(("y", "z_lo")) * full_width
    scale = lax.rsqrt(total_power / entries + 1e-05)
    own_spec = lax.reduce_precision(spectrum * scale[:, None], exponent_bits=8, mantissa_bits=7)
    panel_scale = lax.all_gather(scale, ("z_hi", "x", "core"), axis=0, tiled=True)

    rows0 = pair_owner[:, 0] * station_count + pair_slot[:, 0]
    rows1 = pair_owner[:, 1] * station_count + pair_slot[:, 1]
    near_raw = panel_raw[rows0]
    far_raw = panel_raw[rows1]
    near_scale = panel_scale[rows0][:, None]
    far_scale = panel_scale[rows1][:, None]
    table = lag_basis(half_width, lag_count)
    obs = observed.reshape(pair_count, lag_count)
    contribs = pair_contributions(
        near_raw, far_raw, near_scale, far_scale, obs,
        win_start[:, None], win_end[:, None], table,
    ).reshape(2 * pair_count, full_width)
    owner_flat = jnp.concatenate([pair_owner[:, 0], pair_owner[:, 1]])
    slot_flat = jnp.concatenate([pair_slot[:, 0], pair_slot[:, 1]])
    position = owner_positions(owner_flat, owners)
    flat_slot = owner_flat * capacity + position
    slot_station = (
        jnp.full((owners * capacity,), station_count, jnp.int32)
        .at[flat_slot]
        .set(slot_flat, unique_indices=True)
    ).reshape(owners, 1, capacity)
    slotted = (
        jnp.zeros((owners * capacity, full_width), jnp.bfloat16)
        .at[flat_slot]
        .set(contribs, unique_indices=True)
    ).reshape(owners, capacity, full_width)
    station_ids = jnp.arange(station_count, dtype=jnp.int32)[None, :, None]
    onehot = (slot_station == station_ids).astype(jnp.bfloat16)
    dense = jnp.einsum(
        "osk,okf->osf", onehot, slotted, preferred_element_type=jnp.float32
    ).astype(jnp.bfloat16).reshape(owners * station_count, full_width)
    core = lax.axis_index("core")
    by_core = dense.reshape(owners // 2, 2, station_count, full_width)
    keep = lax.dynamic_index_in_dim(by_core, core, axis=1, keepdims=False)
    give = lax.dynamic_index_in_dim(by_core, 1 - core, axis=1, keepdims=False)
    taken = lax.ppermute(give, "core", perm=[(0, 1), (1, 0)])
    chip_sum = (keep.astype(jnp.float32) + taken.astype(jnp.float32)).astype(jnp.bfloat16)
    summed = lax.psum_scatter(
        chip_sum.reshape(owners // 2 * station_count, full_width),
        ("z_hi", "x"),
        scatter_dimension=0,
        tiled=True,
    )
    return finish(summed, own_spec, band_count)


def solution(mesh):
    fine = jax.sharding.Mesh(
        mesh.devices.reshape(2, 4, 2, 4, 2), ("z_hi", "x", "core", "y", "z_lo")
    )
    pairs = ("z_hi", "x", "core")
    band = ("y", "z_lo")
    return jax.shard_map(
        shards,
        mesh=fine,
        in_specs=(
            P(pairs, band, None),
            P(pairs, band, None),
            P(pairs, None),
            P(pairs, None),
            P(pairs),
            P(pairs),
        ),
        out_specs=P(pairs, band, None),
        check_vma=False,
    )
```

```python
import math

import jax
import jax.numpy as jnp
from jax import lax
from jax.sharding import PartitionSpec as P
from jax.experimental import pallas as pl
from jax.experimental.pallas import tpu as pltpu


def lag_basis(half_width, lag_count):
    freqs = jnp.arange(half_width, dtype=jnp.int32)
    lag_index = jnp.arange(lag_count, dtype=jnp.int32)
    phases = (freqs[:, None] * lag_index[None, :] % lag_count).astype(jnp.float32) * (
        2.0 * math.pi / lag_count
    )
    factor = 1.0 / math.sqrt(lag_count)
    return jnp.concatenate([jnp.cos(phases) * factor, -jnp.sin(phases) * factor], axis=0).astype(
        jnp.bfloat16
    )


def owner_positions(owner_flat, owner_count):
    onehot = (owner_flat[:, None] == jnp.arange(owner_count, dtype=jnp.int32)[None, :]).astype(
        jnp.int32
    )
    before = jnp.cumsum(onehot, axis=0) - onehot
    return jnp.sum(before * onehot, axis=1)


def round_bf16(x):
    return x.astype(jnp.bfloat16).astype(jnp.float32)


def pair_kernel(near_ref, far_ref, ns_ref, fs_ref, obs_ref, ws_ref, we_ref, table_ref, out_ref):
    half = near_ref.shape[1] // 2
    near = round_bf16(near_ref[...].astype(jnp.float32) * ns_ref[...])
    far = round_bf16(far_ref[...].astype(jnp.float32) * fs_ref[...])
    near_re, near_im = near[:, :half], near[:, half:]
    far_re, far_im = far[:, :half], far[:, half:]
    cross_re = (near_re * far_re + near_im * far_im).astype(jnp.bfloat16)
    cross_im = (near_im * far_re - near_re * far_im).astype(jnp.bfloat16)
    tab_re = table_ref[:half, :]
    tab_im = table_ref[half:, :]
    lagged = jnp.dot(cross_re, tab_re, preferred_element_type=jnp.float32) + jnp.dot(
        cross_im, tab_im, preferred_element_type=jnp.float32
    )
    lag = lax.broadcasted_iota(jnp.int32, lagged.shape, 1)
    inside = (lag >= ws_ref[...]) & (lag < we_ref[...])
    residual = jnp.where(inside, lagged - obs_ref[...].astype(jnp.float32), 0.0).astype(
        jnp.bfloat16
    )
    dims = (((1,), (1,)), ((), ()))
    adj_re = lax.dot_general(residual, tab_re, dims, preferred_element_type=jnp.float32)
    adj_im = lax.dot_general(residual, tab_im, dims, preferred_element_type=jnp.float32)
    out_ref[0, :, :half] = (adj_re * far_re - adj_im * far_im).astype(jnp.bfloat16)
    out_ref[0, :, half:] = (adj_re * far_im + adj_im * far_re).astype(jnp.bfloat16)
    out_ref[1, :, :half] = (adj_re * near_re + adj_im * near_im).astype(jnp.bfloat16)
    out_ref[1, :, half:] = (adj_re * near_im - adj_im * near_re).astype(jnp.bfloat16)


def pair_contributions(near_raw, far_raw, near_scale, far_scale, obs, ws, we, table, block=512):
    pairs, width = near_raw.shape
    lags = obs.shape[1]
    row = lambda i: (i, 0)
    return pl.pallas_call(
        pair_kernel,
        grid=(pairs // block,),
        in_specs=[
            pl.BlockSpec((block, width), row),
            pl.BlockSpec((block, width), row),
            pl.BlockSpec((block, 1), row),
            pl.BlockSpec((block, 1), row),
            pl.BlockSpec((block, lags), row),
            pl.BlockSpec((block, 1), row),
            pl.BlockSpec((block, 1), row),
            pl.BlockSpec((width, lags), lambda i: (0, 0)),
        ],
        out_specs=pl.BlockSpec((2, block, width), lambda i: (0, i, 0)),
        out_shape=jax.ShapeDtypeStruct((2, pairs, width), jnp.bfloat16),
        compiler_params=pltpu.CompilerParams(vmem_limit_bytes=48 * 1024 * 1024),
    )(near_raw, far_raw, near_scale, far_scale, obs, ws, we, table)


def finish_kernel(summed_ref, own_ref, out_ref):
    half = own_ref.shape[1] // 2
    summed = summed_ref[...].astype(jnp.float32)
    own = own_ref[...]
    value = 0.25 * (summed[:, :half] * own[:, :half] + summed[:, half:] * own[:, half:])
    out_ref[...] = value.reshape(out_ref.shape)


def finish(summed, own_spec, band_count):
    stations, width = own_spec.shape
    return pl.pallas_call(
        finish_kernel,
        out_shape=jax.ShapeDtypeStruct((stations, band_count, width // 2), jnp.float32),
    )(summed, own_spec)


def shards(spectra, observed, pair_owner, pair_slot, win_start, win_end):
    owners = lax.axis_size(("z_hi", "x", "core"))
    station_count = spectra.shape[0]
    band_count = spectra.shape[1]
    full_width = spectra.shape[2]
    half_width = full_width // 2
    pair_count = observed.shape[0]
    lag_count = observed.shape[2]
    capacity = 3 * pair_count // owners
    raw = spectra.reshape(station_count, full_width)
    panel_raw = lax.all_gather(raw, ("z_hi", "x", "core"), axis=0, tiled=True)
    spectrum = raw.astype(jnp.float32)
    local_power = jnp.sum(spectrum * spectrum, axis=1)
    total_power = lax.psum(local_power, ("y", "z_lo"))
    entries = band_count * lax.axis_size(("y", "z_lo")) * full_width
    scale = lax.rsqrt(total_power / entries + 1e-05)
    own_spec = lax.reduce_precision(spectrum * scale[:, None], exponent_bits=8, mantissa_bits=7)
    panel_scale = lax.all_gather(scale, ("z_hi", "x", "core"), axis=0, tiled=True)

    rows0 = pair_owner[:, 0] * station_count + pair_slot[:, 0]
    rows1 = pair_owner[:, 1] * station_count + pair_slot[:, 1]
    near_raw = panel_raw[rows0]
    far_raw = panel_raw[rows1]
    near_scale = panel_scale[rows0][:, None]
    far_scale = panel_scale[rows1][:, None]
    table = lag_basis(half_width, lag_count)
    obs = observed.reshape(pair_count, lag_count)
    contribs = pair_contributions(
        near_raw, far_raw, near_scale, far_scale, obs,
        win_start[:, None], win_end[:, None], table,
    ).reshape(2 * pair_count, full_width)
    core = lax.axis_index("core")
    owner_flat = jnp.concatenate([pair_owner[:, 0], pair_owner[:, 1]])
    owner_flat = ((owner_flat % 2) ^ core) * (owners // 2) + owner_flat // 2
    slot_flat = jnp.concatenate([pair_slot[:, 0], pair_slot[:, 1]])
    position = owner_positions(owner_flat, owners)
    flat_slot = owner_flat * capacity + position
    slot_station = (
        jnp.full((owners * capacity,), station_count, jnp.int32)
        .at[flat_slot]
        .set(slot_flat, unique_indices=True)
    ).reshape(owners, 1, capacity)
    slotted = (
        jnp.zeros((owners * capacity, full_width), jnp.bfloat16)
        .at[flat_slot]
        .set(contribs, unique_indices=True)
    ).reshape(owners, capacity, full_width)
    station_ids = jnp.arange(station_count, dtype=jnp.int32)[None, :, None]
    onehot = (slot_station == station_ids).astype(jnp.bfloat16)
    half = owners // 2
    give = jnp.einsum(
        "osk,okf->osf", onehot[half:], slotted[half:], preferred_element_type=jnp.float32
    ).astype(jnp.bfloat16)
    taken = lax.ppermute(give, "core", perm=[(0, 1), (1, 0)])
    keep = jnp.einsum(
        "osk,okf->osf", onehot[:half], slotted[:half], preferred_element_type=jnp.float32
    )
    chip_sum = (keep + taken.astype(jnp.float32)).astype(jnp.bfloat16)
    summed = lax.psum_scatter(
        chip_sum.reshape(owners // 2 * station_count, full_width),
        ("z_hi", "x"),
        scatter_dimension=0,
        tiled=True,
    )
    return finish(summed, own_spec, band_count)


def solution(mesh):
    fine = jax.sharding.Mesh(
        mesh.devices.reshape(2, 4, 2, 4, 2), ("z_hi", "x", "core", "y", "z_lo")
    )
    pairs = ("z_hi", "x", "core")
    band = ("y", "z_lo")
    return jax.shard_map(
        shards,
        mesh=fine,
        in_specs=(
            P(pairs, band, None),
            P(pairs, band, None),
            P(pairs, None),
            P(pairs, None),
            P(pairs),
            P(pairs),
        ),
        out_specs=P(pairs, band, None),
        check_vma=False,
    )
```

```python
import math

import jax
import jax.numpy as jnp
from jax import lax
from jax.sharding import PartitionSpec as P
from jax.experimental import pallas as pl
from jax.experimental.pallas import tpu as pltpu


def lag_basis(half_width, lag_count):
    freqs = jnp.arange(half_width, dtype=jnp.int32)
    lag_index = jnp.arange(lag_count, dtype=jnp.int32)
    phases = (freqs[:, None] * lag_index[None, :] % lag_count).astype(jnp.float32) * (
        2.0 * math.pi / lag_count
    )
    factor = 1.0 / math.sqrt(lag_count)
    return jnp.concatenate([jnp.cos(phases) * factor, -jnp.sin(phases) * factor], axis=0).astype(
        jnp.bfloat16
    )


def owner_positions(owner_flat, owner_count):
    onehot = (owner_flat[:, None] == jnp.arange(owner_count, dtype=jnp.int32)[None, :]).astype(
        jnp.int32
    )
    before = jnp.cumsum(onehot, axis=0) - onehot
    return jnp.sum(before * onehot, axis=1)


def round_bf16(x):
    return x.astype(jnp.bfloat16).astype(jnp.float32)


def pair_kernel(near_ref, far_ref, ns_ref, fs_ref, obs_ref, ws_ref, we_ref, table_ref, out_ref):
    half = near_ref.shape[1] // 2
    near = round_bf16(near_ref[...].astype(jnp.float32) * ns_ref[...])
    far = round_bf16(far_ref[...].astype(jnp.float32) * fs_ref[...])
    near_re, near_im = near[:, :half], near[:, half:]
    far_re, far_im = far[:, :half], far[:, half:]
    cross_re = (near_re * far_re + near_im * far_im).astype(jnp.bfloat16)
    cross_im = (near_im * far_re - near_re * far_im).astype(jnp.bfloat16)
    tab_re = table_ref[:half, :]
    tab_im = table_ref[half:, :]
    lagged = jnp.dot(cross_re, tab_re, preferred_element_type=jnp.float32) + jnp.dot(
        cross_im, tab_im, preferred_element_type=jnp.float32
    )
    lag = lax.broadcasted_iota(jnp.int32, lagged.shape, 1)
    inside = (lag >= ws_ref[...]) & (lag < we_ref[...])
    residual = jnp.where(inside, lagged - obs_ref[...].astype(jnp.float32), 0.0).astype(
        jnp.bfloat16
    )
    dims = (((1,), (1,)), ((), ()))
    adj_re = lax.dot_general(residual, tab_re, dims, preferred_element_type=jnp.float32)
    adj_im = lax.dot_general(residual, tab_im, dims, preferred_element_type=jnp.float32)
    out_ref[0, :, :half] = (adj_re * far_re - adj_im * far_im).astype(jnp.bfloat16)
    out_ref[0, :, half:] = (adj_re * far_im + adj_im * far_re).astype(jnp.bfloat16)
    out_ref[1, :, :half] = (adj_re * near_re + adj_im * near_im).astype(jnp.bfloat16)
    out_ref[1, :, half:] = (adj_re * near_im - adj_im * near_re).astype(jnp.bfloat16)


def pair_contributions(near_raw, far_raw, near_scale, far_scale, obs, ws, we, table, block=512):
    pairs, width = near_raw.shape
    lags = obs.shape[1]
    row = lambda i: (i, 0)
    return pl.pallas_call(
        pair_kernel,
        grid=(pairs // block,),
        in_specs=[
            pl.BlockSpec((block, width), row),
            pl.BlockSpec((block, width), row),
            pl.BlockSpec((block, 1), row),
            pl.BlockSpec((block, 1), row),
            pl.BlockSpec((block, lags), row),
            pl.BlockSpec((block, 1), row),
            pl.BlockSpec((block, 1), row),
            pl.BlockSpec((width, lags), lambda i: (0, 0)),
        ],
        out_specs=pl.BlockSpec((2, block, width), lambda i: (0, i, 0)),
        out_shape=jax.ShapeDtypeStruct((2, pairs, width), jnp.bfloat16),
        compiler_params=pltpu.CompilerParams(vmem_limit_bytes=48 * 1024 * 1024),
    )(near_raw, far_raw, near_scale, far_scale, obs, ws, we, table)


def finish_kernel(summed_ref, own_ref, out_ref):
    half = own_ref.shape[1] // 2
    summed = summed_ref[...].astype(jnp.float32)
    own = own_ref[...]
    value = 0.25 * (summed[:, :half] * own[:, :half] + summed[:, half:] * own[:, half:])
    out_ref[...] = value.reshape(out_ref.shape)


def finish(summed, own_spec, band_count):
    stations, width = own_spec.shape
    return pl.pallas_call(
        finish_kernel,
        out_shape=jax.ShapeDtypeStruct((stations, band_count, width // 2), jnp.float32),
    )(summed, own_spec)


def shards(spectra, observed, pair_owner, pair_slot, win_start, win_end):
    owners = lax.axis_size(("z_hi", "x", "core"))
    station_count = spectra.shape[0]
    band_count = spectra.shape[1]
    full_width = spectra.shape[2]
    half_width = full_width // 2
    pair_count = observed.shape[0]
    lag_count = observed.shape[2]
    capacity = 3 * pair_count // owners
    raw = spectra.reshape(station_count, full_width)
    panel_raw = lax.all_gather(raw, ("z_hi", "x", "core"), axis=0, tiled=True)
    spectrum = raw.astype(jnp.float32)
    local_power = jnp.sum(spectrum * spectrum, axis=1)
    total_power = lax.psum(local_power, ("y", "z_lo"))
    entries = band_count * lax.axis_size(("y", "z_lo")) * full_width
    scale = lax.rsqrt(total_power / entries + 1e-05)
    own_spec = lax.reduce_precision(spectrum * scale[:, None], exponent_bits=8, mantissa_bits=7)
    panel_scale = lax.all_gather(scale, ("z_hi", "x", "core"), axis=0, tiled=True)

    rows0 = pair_owner[:, 0] * station_count + pair_slot[:, 0]
    rows1 = pair_owner[:, 1] * station_count + pair_slot[:, 1]
    near_raw = panel_raw[rows0]
    far_raw = panel_raw[rows1]
    near_scale = panel_scale[rows0][:, None]
    far_scale = panel_scale[rows1][:, None]
    table = lag_basis(half_width, lag_count)
    obs = observed.reshape(pair_count, lag_count)
    contribs = pair_contributions(
        near_raw, far_raw, near_scale, far_scale, obs,
        win_start[:, None], win_end[:, None], table,
    ).reshape(2 * pair_count, full_width)
    core = lax.axis_index("core")
    owner_flat = jnp.concatenate([pair_owner[:, 0], pair_owner[:, 1]])
    owner_flat = ((owner_flat % 2) ^ core) * (owners // 2) + owner_flat // 2
    slot_flat = jnp.concatenate([pair_slot[:, 0], pair_slot[:, 1]])
    position = owner_positions(owner_flat, owners)
    flat_slot = owner_flat * capacity + position
    slot_station = (
        jnp.full((owners * capacity,), station_count, jnp.int32)
        .at[flat_slot]
        .set(slot_flat, unique_indices=True)
    ).reshape(owners, 1, capacity)
    slotted = (
        jnp.zeros((owners * capacity, full_width), jnp.bfloat16)
        .at[flat_slot]
        .set(contribs, unique_indices=True)
    ).reshape(owners, capacity, full_width)
    station_ids = jnp.arange(station_count, dtype=jnp.int32)[None, :, None]
    onehot = (slot_station == station_ids).astype(jnp.bfloat16)
    half = owners // 2
    quarter = half // 2
    taken = []
    for start in (half, half + quarter):
        give = jnp.einsum(
            "osk,okf->osf",
            onehot[start:start + quarter],
            slotted[start:start + quarter],
            preferred_element_type=jnp.float32,
        ).astype(jnp.bfloat16)
        taken.append(lax.ppermute(give, "core", perm=[(0, 1), (1, 0)]))
    taken = jnp.concatenate(taken, axis=0)
    keep = jnp.einsum(
        "osk,okf->osf", onehot[:half], slotted[:half], preferred_element_type=jnp.float32
    )
    chip_sum = (keep + taken.astype(jnp.float32)).astype(jnp.bfloat16)
    summed = lax.psum_scatter(
        chip_sum.reshape(owners // 2 * station_count, full_width),
        ("z_hi", "x"),
        scatter_dimension=0,
        tiled=True,
    )
    return finish(summed, own_spec, band_count)


def solution(mesh):
    fine = jax.sharding.Mesh(
        mesh.devices.reshape(2, 4, 2, 4, 2), ("z_hi", "x", "core", "y", "z_lo")
    )
    pairs = ("z_hi", "x", "core")
    band = ("y", "z_lo")
    return jax.shard_map(
        shards,
        mesh=fine,
        in_specs=(
            P(pairs, band, None),
            P(pairs, band, None),
            P(pairs, None),
            P(pairs, None),
            P(pairs),
            P(pairs),
        ),
        out_specs=P(pairs, band, None),
        check_vma=False,
    )
```

```python
import math

import jax
import jax.numpy as jnp
from jax import lax
from jax.sharding import PartitionSpec as P
from jax.experimental import pallas as pl
from jax.experimental.pallas import tpu as pltpu


def lag_basis(half_width, lag_count):
    freqs = jnp.arange(half_width, dtype=jnp.int32)
    lag_index = jnp.arange(lag_count, dtype=jnp.int32)
    phases = (freqs[:, None] * lag_index[None, :] % lag_count).astype(jnp.float32) * (
        2.0 * math.pi / lag_count
    )
    factor = 1.0 / math.sqrt(lag_count)
    return jnp.concatenate([jnp.cos(phases) * factor, -jnp.sin(phases) * factor], axis=0).astype(
        jnp.bfloat16
    )


def owner_positions(owner_flat, owner_count):
    onehot = (owner_flat[:, None] == jnp.arange(owner_count, dtype=jnp.int32)[None, :]).astype(
        jnp.int32
    )
    before = jnp.cumsum(onehot, axis=0) - onehot
    return jnp.sum(before * onehot, axis=1)


def round_bf16(x):
    return x.astype(jnp.bfloat16).astype(jnp.float32)


def pair_kernel(near_ref, far_ref, ns_ref, fs_ref, obs_ref, ws_ref, we_ref, table_ref, out_ref):
    half = near_ref.shape[1] // 2
    near = round_bf16(near_ref[...].astype(jnp.float32) * ns_ref[...])
    far = round_bf16(far_ref[...].astype(jnp.float32) * fs_ref[...])
    near_re, near_im = near[:, :half], near[:, half:]
    far_re, far_im = far[:, :half], far[:, half:]
    cross_re = (near_re * far_re + near_im * far_im).astype(jnp.bfloat16)
    cross_im = (near_im * far_re - near_re * far_im).astype(jnp.bfloat16)
    tab_re = table_ref[:half, :]
    tab_im = table_ref[half:, :]
    lagged = jnp.dot(cross_re, tab_re, preferred_element_type=jnp.float32) + jnp.dot(
        cross_im, tab_im, preferred_element_type=jnp.float32
    )
    lag = lax.broadcasted_iota(jnp.int32, lagged.shape, 1)
    inside = (lag >= ws_ref[...]) & (lag < we_ref[...])
    residual = jnp.where(inside, lagged - obs_ref[...].astype(jnp.float32), 0.0).astype(
        jnp.bfloat16
    )
    dims = (((1,), (1,)), ((), ()))
    adj_re = lax.dot_general(residual, tab_re, dims, preferred_element_type=jnp.float32)
    adj_im = lax.dot_general(residual, tab_im, dims, preferred_element_type=jnp.float32)
    out_ref[0, :, :half] = (adj_re * far_re - adj_im * far_im).astype(jnp.bfloat16)
    out_ref[0, :, half:] = (adj_re * far_im + adj_im * far_re).astype(jnp.bfloat16)
    out_ref[1, :, :half] = (adj_re * near_re + adj_im * near_im).astype(jnp.bfloat16)
    out_ref[1, :, half:] = (adj_re * near_im - adj_im * near_re).astype(jnp.bfloat16)


def pair_contributions(near_raw, far_raw, near_scale, far_scale, obs, ws, we, table, block=512):
    pairs, width = near_raw.shape
    lags = obs.shape[1]
    row = lambda i: (i, 0)
    return pl.pallas_call(
        pair_kernel,
        grid=(pairs // block,),
        in_specs=[
            pl.BlockSpec((block, width), row),
            pl.BlockSpec((block, width), row),
            pl.BlockSpec((block, 1), row),
            pl.BlockSpec((block, 1), row),
            pl.BlockSpec((block, lags), row),
            pl.BlockSpec((block, 1), row),
            pl.BlockSpec((block, 1), row),
            pl.BlockSpec((width, lags), lambda i: (0, 0)),
        ],
        out_specs=pl.BlockSpec((2, block, width), lambda i: (0, i, 0)),
        out_shape=jax.ShapeDtypeStruct((2, pairs, width), jnp.bfloat16),
        compiler_params=pltpu.CompilerParams(vmem_limit_bytes=48 * 1024 * 1024),
    )(near_raw, far_raw, near_scale, far_scale, obs, ws, we, table)


def finish_kernel(summed_ref, own_ref, out_ref):
    half = own_ref.shape[1] // 2
    summed = summed_ref[...].astype(jnp.float32)
    own = own_ref[...]
    value = 0.25 * (summed[:, :half] * own[:, :half] + summed[:, half:] * own[:, half:])
    out_ref[...] = value.reshape(out_ref.shape)


def finish(summed, own_spec, band_count):
    stations, width = own_spec.shape
    return pl.pallas_call(
        finish_kernel,
        out_shape=jax.ShapeDtypeStruct((stations, band_count, width // 2), jnp.float32),
    )(summed, own_spec)


def shards(spectra, observed, pair_owner, pair_slot, win_start, win_end):
    owners = lax.axis_size(("z_hi", "x", "core"))
    station_count = spectra.shape[0]
    band_count = spectra.shape[1]
    full_width = spectra.shape[2]
    half_width = full_width // 2
    pair_count = observed.shape[0]
    lag_count = observed.shape[2]
    capacity = 3 * pair_count // owners
    raw = spectra.reshape(station_count, full_width)
    panel_raw = lax.all_gather(raw, ("z_hi", "x", "core"), axis=0, tiled=True)
    spectrum = raw.astype(jnp.float32)
    local_power = jnp.sum(spectrum * spectrum, axis=1)
    total_power = lax.psum(local_power, ("y", "z_lo"))
    entries = band_count * lax.axis_size(("y", "z_lo")) * full_width
    scale = lax.rsqrt(total_power / entries + 1e-05)
    own_spec = lax.reduce_precision(spectrum * scale[:, None], exponent_bits=8, mantissa_bits=7)
    panel_scale = lax.all_gather(scale, ("z_hi", "x", "core"), axis=0, tiled=True)

    rows0 = pair_owner[:, 0] * station_count + pair_slot[:, 0]
    rows1 = pair_owner[:, 1] * station_count + pair_slot[:, 1]
    near_raw = panel_raw[rows0]
    far_raw = panel_raw[rows1]
    near_scale = panel_scale[rows0][:, None]
    far_scale = panel_scale[rows1][:, None]
    table = lag_basis(half_width, lag_count)
    obs = observed.reshape(pair_count, lag_count)
    contribs = pair_contributions(
        near_raw, far_raw, near_scale, far_scale, obs,
        win_start[:, None], win_end[:, None], table,
    ).reshape(2 * pair_count, full_width)
    core = lax.axis_index("core")
    owner_flat = jnp.concatenate([pair_owner[:, 0], pair_owner[:, 1]])
    owner_flat = ((owner_flat % 2) ^ core) * (owners // 2) + owner_flat // 2
    slot_flat = jnp.concatenate([pair_slot[:, 0], pair_slot[:, 1]])
    position = owner_positions(owner_flat, owners)
    flat_slot = owner_flat * capacity + position
    slot_station = (
        jnp.full((owners * capacity,), station_count, jnp.int32)
        .at[flat_slot]
        .set(slot_flat, unique_indices=True)
    ).reshape(owners, 1, capacity)
    slotted = (
        jnp.zeros((owners * capacity, full_width), jnp.bfloat16)
        .at[flat_slot]
        .set(contribs, unique_indices=True)
    ).reshape(owners, capacity, full_width)
    station_ids = jnp.arange(station_count, dtype=jnp.int32)[None, :, None]
    onehot = (slot_station == station_ids).astype(jnp.bfloat16)
    half = owners // 2
    quarter = half // 4
    taken = []
    for start in range(half, owners, quarter):
        give = jnp.einsum(
            "osk,okf->osf",
            onehot[start:start + quarter],
            slotted[start:start + quarter],
            preferred_element_type=jnp.float32,
        ).astype(jnp.bfloat16)
        taken.append(lax.ppermute(give, "core", perm=[(0, 1), (1, 0)]))
    taken = jnp.concatenate(taken, axis=0)
    keep = jnp.einsum(
        "osk,okf->osf", onehot[:half], slotted[:half], preferred_element_type=jnp.float32
    )
    chip_sum = (keep + taken.astype(jnp.float32)).astype(jnp.bfloat16)
    summed = lax.psum_scatter(
        chip_sum.reshape(owners // 2 * station_count, full_width),
        ("z_hi", "x"),
        scatter_dimension=0,
        tiled=True,
    )
    return finish(summed, own_spec, band_count)


def solution(mesh):
    fine = jax.sharding.Mesh(
        mesh.devices.reshape(2, 4, 2, 4, 2), ("z_hi", "x", "core", "y", "z_lo")
    )
    pairs = ("z_hi", "x", "core")
    band = ("y", "z_lo")
    return jax.shard_map(
        shards,
        mesh=fine,
        in_specs=(
            P(pairs, band, None),
            P(pairs, band, None),
            P(pairs, None),
            P(pairs, None),
            P(pairs),
            P(pairs),
        ),
        out_specs=P(pairs, band, None),
        check_vma=False,
    )
```

```python
import math

import jax
import jax.numpy as jnp
from jax import lax
from jax.sharding import PartitionSpec as P
from jax.experimental import pallas as pl
from jax.experimental.pallas import tpu as pltpu


def lag_basis(half_width, lag_count):
    freqs = jnp.arange(half_width, dtype=jnp.int32)
    lag_index = jnp.arange(lag_count, dtype=jnp.int32)
    phases = (freqs[:, None] * lag_index[None, :] % lag_count).astype(jnp.float32) * (
        2.0 * math.pi / lag_count
    )
    factor = 1.0 / math.sqrt(lag_count)
    return jnp.concatenate([jnp.cos(phases) * factor, -jnp.sin(phases) * factor], axis=0).astype(
        jnp.bfloat16
    )


def owner_positions(owner_flat, owner_count):
    onehot = (owner_flat[:, None] == jnp.arange(owner_count, dtype=jnp.int32)[None, :]).astype(
        jnp.int32
    )
    before = jnp.cumsum(onehot, axis=0) - onehot
    return jnp.sum(before * onehot, axis=1)


def round_bf16(x):
    return x.astype(jnp.bfloat16).astype(jnp.float32)


def pair_kernel(near_ref, far_ref, ns_ref, fs_ref, obs_ref, ws_ref, we_ref, table_ref, out_ref):
    half = near_ref.shape[1] // 2
    near = round_bf16(near_ref[...].astype(jnp.float32) * ns_ref[...])
    far = round_bf16(far_ref[...].astype(jnp.float32) * fs_ref[...])
    near_re, near_im = near[:, :half], near[:, half:]
    far_re, far_im = far[:, :half], far[:, half:]
    cross_re = (near_re * far_re + near_im * far_im).astype(jnp.bfloat16)
    cross_im = (near_im * far_re - near_re * far_im).astype(jnp.bfloat16)
    tab_re = table_ref[:half, :]
    tab_im = table_ref[half:, :]
    lagged = jnp.dot(cross_re, tab_re, preferred_element_type=jnp.float32) + jnp.dot(
        cross_im, tab_im, preferred_element_type=jnp.float32
    )
    lag = lax.broadcasted_iota(jnp.int32, lagged.shape, 1)
    inside = (lag >= ws_ref[...]) & (lag < we_ref[...])
    residual = jnp.where(inside, lagged - obs_ref[...].astype(jnp.float32), 0.0).astype(
        jnp.bfloat16
    )
    dims = (((1,), (1,)), ((), ()))
    adj_re = lax.dot_general(residual, tab_re, dims, preferred_element_type=jnp.float32)
    adj_im = lax.dot_general(residual, tab_im, dims, preferred_element_type=jnp.float32)
    out_ref[0, :, :half] = (adj_re * far_re - adj_im * far_im).astype(jnp.bfloat16)
    out_ref[0, :, half:] = (adj_re * far_im + adj_im * far_re).astype(jnp.bfloat16)
    out_ref[1, :, :half] = (adj_re * near_re + adj_im * near_im).astype(jnp.bfloat16)
    out_ref[1, :, half:] = (adj_re * near_im - adj_im * near_re).astype(jnp.bfloat16)


def pair_contributions(near_raw, far_raw, near_scale, far_scale, obs, ws, we, table, block=512):
    pairs, width = near_raw.shape
    lags = obs.shape[1]
    row = lambda i: (i, 0)
    return pl.pallas_call(
        pair_kernel,
        grid=(pairs // block,),
        in_specs=[
            pl.BlockSpec((block, width), row),
            pl.BlockSpec((block, width), row),
            pl.BlockSpec((block, 1), row),
            pl.BlockSpec((block, 1), row),
            pl.BlockSpec((block, lags), row),
            pl.BlockSpec((block, 1), row),
            pl.BlockSpec((block, 1), row),
            pl.BlockSpec((width, lags), lambda i: (0, 0)),
        ],
        out_specs=pl.BlockSpec((2, block, width), lambda i: (0, i, 0)),
        out_shape=jax.ShapeDtypeStruct((2, pairs, width), jnp.bfloat16),
        compiler_params=pltpu.CompilerParams(vmem_limit_bytes=48 * 1024 * 1024),
    )(near_raw, far_raw, near_scale, far_scale, obs, ws, we, table)


def finish_kernel(summed_ref, own_ref, out_ref):
    half = own_ref.shape[1] // 2
    summed = summed_ref[...].astype(jnp.float32)
    own = own_ref[...]
    value = 0.25 * (summed[:, :half] * own[:, :half] + summed[:, half:] * own[:, half:])
    out_ref[...] = value.reshape(out_ref.shape)


def finish(summed, own_spec, band_count):
    stations, width = own_spec.shape
    return pl.pallas_call(
        finish_kernel,
        out_shape=jax.ShapeDtypeStruct((stations, band_count, width // 2), jnp.float32),
    )(summed, own_spec)


def shards(spectra, observed, pair_owner, pair_slot, win_start, win_end):
    owners = lax.axis_size(("z_hi", "x", "core"))
    station_count = spectra.shape[0]
    band_count = spectra.shape[1]
    full_width = spectra.shape[2]
    half_width = full_width // 2
    pair_count = observed.shape[0]
    lag_count = observed.shape[2]
    capacity = 3 * pair_count // owners
    raw = spectra.reshape(station_count, full_width)
    panel_raw = lax.all_gather(raw, ("z_hi", "x", "core"), axis=0, tiled=True)
    spectrum = raw.astype(jnp.float32)
    local_power = jnp.sum(spectrum * spectrum, axis=1)
    total_power = lax.psum(local_power, ("y", "z_lo"))
    entries = band_count * lax.axis_size(("y", "z_lo")) * full_width
    scale = lax.rsqrt(total_power / entries + 1e-05)
    own_spec = lax.reduce_precision(spectrum * scale[:, None], exponent_bits=8, mantissa_bits=7)
    panel_scale = lax.all_gather(scale, ("z_hi", "x", "core"), axis=0, tiled=True)

    rows0 = pair_owner[:, 0] * station_count + pair_slot[:, 0]
    rows1 = pair_owner[:, 1] * station_count + pair_slot[:, 1]
    near_raw = panel_raw[rows0]
    far_raw = panel_raw[rows1]
    near_scale = panel_scale[rows0][:, None]
    far_scale = panel_scale[rows1][:, None]
    table = lag_basis(half_width, lag_count)
    obs = observed.reshape(pair_count, lag_count)
    contribs = pair_contributions(
        near_raw, far_raw, near_scale, far_scale, obs,
        win_start[:, None], win_end[:, None], table,
    ).reshape(2 * pair_count, full_width)
    core = lax.axis_index("core")
    owner_flat = jnp.concatenate([pair_owner[:, 0], pair_owner[:, 1]])
    owner_flat = ((owner_flat % 2) ^ core) * (owners // 2) + owner_flat // 2
    slot_flat = jnp.concatenate([pair_slot[:, 0], pair_slot[:, 1]])
    position = owner_positions(owner_flat, owners)
    flat_slot = owner_flat * capacity + position
    slot_station = (
        jnp.full((owners * capacity,), station_count, jnp.int32)
        .at[flat_slot]
        .set(slot_flat, unique_indices=True)
    ).reshape(owners, 1, capacity)
    slotted = (
        jnp.zeros((owners * capacity, full_width), jnp.bfloat16)
        .at[flat_slot]
        .set(contribs, unique_indices=True)
    ).reshape(owners, capacity, full_width)
    station_ids = jnp.arange(station_count, dtype=jnp.int32)[None, :, None]
    onehot = (slot_station == station_ids).astype(jnp.bfloat16)
    half = owners // 2
    quarter = half // 8
    taken = []
    for start in range(half, owners, quarter):
        give = jnp.einsum(
            "osk,okf->osf",
            onehot[start:start + quarter],
            slotted[start:start + quarter],
            preferred_element_type=jnp.float32,
        ).astype(jnp.bfloat16)
        taken.append(lax.ppermute(give, "core", perm=[(0, 1), (1, 0)]))
    taken = jnp.concatenate(taken, axis=0)
    keep = jnp.einsum(
        "osk,okf->osf", onehot[:half], slotted[:half], preferred_element_type=jnp.float32
    )
    chip_sum = (keep + taken.astype(jnp.float32)).astype(jnp.bfloat16)
    summed = lax.psum_scatter(
        chip_sum.reshape(owners // 2 * station_count, full_width),
        ("z_hi", "x"),
        scatter_dimension=0,
        tiled=True,
    )
    return finish(summed, own_spec, band_count)


def solution(mesh):
    fine = jax.sharding.Mesh(
        mesh.devices.reshape(2, 4, 2, 4, 2), ("z_hi", "x", "core", "y", "z_lo")
    )
    pairs = ("z_hi", "x", "core")
    band = ("y", "z_lo")
    return jax.shard_map(
        shards,
        mesh=fine,
        in_specs=(
            P(pairs, band, None),
            P(pairs, band, None),
            P(pairs, None),
            P(pairs, None),
            P(pairs),
            P(pairs),
        ),
        out_specs=P(pairs, band, None),
        check_vma=False,
    )
```

```python
import math

import jax
import jax.numpy as jnp
from jax import lax
from jax.sharding import PartitionSpec as P
from jax.experimental import pallas as pl
from jax.experimental.pallas import tpu as pltpu


def lag_basis(half_width, lag_count):
    freqs = jnp.arange(half_width, dtype=jnp.int32)
    lag_index = jnp.arange(lag_count, dtype=jnp.int32)
    phases = (freqs[:, None] * lag_index[None, :] % lag_count).astype(jnp.float32) * (
        2.0 * math.pi / lag_count
    )
    factor = 1.0 / math.sqrt(lag_count)
    return jnp.concatenate([jnp.cos(phases) * factor, -jnp.sin(phases) * factor], axis=0).astype(
        jnp.bfloat16
    )


def owner_positions(owner_flat, owner_count):
    onehot = (owner_flat[:, None] == jnp.arange(owner_count, dtype=jnp.int32)[None, :]).astype(
        jnp.int32
    )
    before = jnp.cumsum(onehot, axis=0) - onehot
    return jnp.sum(before * onehot, axis=1)


def round_bf16(x):
    return x.astype(jnp.bfloat16).astype(jnp.float32)


def pair_kernel(near_ref, far_ref, ns_ref, fs_ref, obs_ref, ws_ref, we_ref, table_ref, out_ref):
    half = near_ref.shape[1] // 2
    near = round_bf16(near_ref[...].astype(jnp.float32) * ns_ref[...])
    far = round_bf16(far_ref[...].astype(jnp.float32) * fs_ref[...])
    near_re, near_im = near[:, :half], near[:, half:]
    far_re, far_im = far[:, :half], far[:, half:]
    cross_re = (near_re * far_re + near_im * far_im).astype(jnp.bfloat16)
    cross_im = (near_im * far_re - near_re * far_im).astype(jnp.bfloat16)
    tab_re = table_ref[:half, :]
    tab_im = table_ref[half:, :]
    lagged = jnp.dot(cross_re, tab_re, preferred_element_type=jnp.float32) + jnp.dot(
        cross_im, tab_im, preferred_element_type=jnp.float32
    )
    lag = lax.broadcasted_iota(jnp.int32, lagged.shape, 1)
    inside = (lag >= ws_ref[...]) & (lag < we_ref[...])
    residual = jnp.where(inside, lagged - obs_ref[...].astype(jnp.float32), 0.0).astype(
        jnp.bfloat16
    )
    dims = (((1,), (1,)), ((), ()))
    adj_re = lax.dot_general(residual, tab_re, dims, preferred_element_type=jnp.float32)
    adj_im = lax.dot_general(residual, tab_im, dims, preferred_element_type=jnp.float32)
    out_ref[0, :, :half] = (adj_re * far_re - adj_im * far_im).astype(jnp.bfloat16)
    out_ref[0, :, half:] = (adj_re * far_im + adj_im * far_re).astype(jnp.bfloat16)
    out_ref[1, :, :half] = (adj_re * near_re + adj_im * near_im).astype(jnp.bfloat16)
    out_ref[1, :, half:] = (adj_re * near_im - adj_im * near_re).astype(jnp.bfloat16)


def pair_contributions(near_raw, far_raw, near_scale, far_scale, obs, ws, we, table, block=512):
    pairs, width = near_raw.shape
    lags = obs.shape[1]
    row = lambda i: (i, 0)
    return pl.pallas_call(
        pair_kernel,
        grid=(pairs // block,),
        in_specs=[
            pl.BlockSpec((block, width), row),
            pl.BlockSpec((block, width), row),
            pl.BlockSpec((block, 1), row),
            pl.BlockSpec((block, 1), row),
            pl.BlockSpec((block, lags), row),
            pl.BlockSpec((block, 1), row),
            pl.BlockSpec((block, 1), row),
            pl.BlockSpec((width, lags), lambda i: (0, 0)),
        ],
        out_specs=pl.BlockSpec((2, block, width), lambda i: (0, i, 0)),
        out_shape=jax.ShapeDtypeStruct((2, pairs, width), jnp.bfloat16),
        compiler_params=pltpu.CompilerParams(vmem_limit_bytes=48 * 1024 * 1024),
    )(near_raw, far_raw, near_scale, far_scale, obs, ws, we, table)


def finish_kernel(summed_ref, own_ref, out_ref):
    half = own_ref.shape[1] // 2
    summed = summed_ref[...].astype(jnp.float32)
    own = own_ref[...]
    value = 0.25 * (summed[:, :half] * own[:, :half] + summed[:, half:] * own[:, half:])
    out_ref[...] = value.reshape(out_ref.shape)


def finish(summed, own_spec, band_count):
    stations, width = own_spec.shape
    return pl.pallas_call(
        finish_kernel,
        out_shape=jax.ShapeDtypeStruct((stations, band_count, width // 2), jnp.float32),
    )(summed, own_spec)


def shards(spectra, observed, pair_owner, pair_slot, win_start, win_end):
    owners = lax.axis_size(("z_hi", "x", "core"))
    station_count = spectra.shape[0]
    band_count = spectra.shape[1]
    full_width = spectra.shape[2]
    half_width = full_width // 2
    pair_count = observed.shape[0]
    lag_count = observed.shape[2]
    capacity = 3 * pair_count // owners
    raw = spectra.reshape(station_count, full_width)
    panel_raw = lax.all_gather(raw, ("z_hi", "x", "core"), axis=0, tiled=True)
    spectrum = raw.astype(jnp.float32)
    local_power = jnp.sum(spectrum * spectrum, axis=1)
    total_power = lax.psum(local_power, ("y", "z_lo"))
    entries = band_count * lax.axis_size(("y", "z_lo")) * full_width
    scale = lax.rsqrt(total_power / entries + 1e-05)
    own_spec = lax.reduce_precision(spectrum * scale[:, None], exponent_bits=8, mantissa_bits=7)
    panel_scale = lax.all_gather(scale, ("z_hi", "x", "core"), axis=0, tiled=True)

    rows0 = pair_owner[:, 0] * station_count + pair_slot[:, 0]
    rows1 = pair_owner[:, 1] * station_count + pair_slot[:, 1]
    near_raw = panel_raw[rows0]
    far_raw = panel_raw[rows1]
    near_scale = panel_scale[rows0][:, None]
    far_scale = panel_scale[rows1][:, None]
    table = lag_basis(half_width, lag_count)
    obs = observed.reshape(pair_count, lag_count)
    contribs = pair_contributions(
        near_raw, far_raw, near_scale, far_scale, obs,
        win_start[:, None], win_end[:, None], table,
    ).reshape(2 * pair_count, full_width)
    core = lax.axis_index("core")
    owner_flat = jnp.concatenate([pair_owner[:, 0], pair_owner[:, 1]])
    owner_flat = ((owner_flat % 2) ^ core) * (owners // 2) + owner_flat // 2
    slot_flat = jnp.concatenate([pair_slot[:, 0], pair_slot[:, 1]])
    position = owner_positions(owner_flat, owners)
    flat_slot = owner_flat * capacity + position
    slot_station = (
        jnp.full((owners * capacity,), station_count, jnp.int32)
        .at[flat_slot]
        .set(slot_flat, unique_indices=True)
    ).reshape(owners, 1, capacity)
    slotted = (
        jnp.zeros((owners * capacity, full_width), jnp.bfloat16)
        .at[flat_slot]
        .set(contribs, unique_indices=True)
    ).reshape(owners, capacity, full_width)
    station_ids = jnp.arange(station_count, dtype=jnp.int32)[None, :, None]
    onehot = (slot_station == station_ids).astype(jnp.bfloat16)
    half = owners // 2
    quarter = half // 4
    taken = []
    for start in range(half, owners, quarter):
        give = jnp.einsum(
            "osk,okf->osf",
            onehot[start:start + quarter],
            slotted[start:start + quarter],
            preferred_element_type=jnp.float32,
        ).astype(jnp.bfloat16)
        taken.append(lax.ppermute(give, "core", perm=[(0, 1), (1, 0)]))
    chip_sum = []
    for part, start in enumerate(range(0, half, quarter)):
        keep = jnp.einsum(
            "osk,okf->osf",
            onehot[start:start + quarter],
            slotted[start:start + quarter],
            preferred_element_type=jnp.float32,
        )
        chip_sum.append((keep + taken[part].astype(jnp.float32)).astype(jnp.bfloat16))
    chip_sum = jnp.concatenate(chip_sum, axis=0)
    summed = lax.psum_scatter(
        chip_sum.reshape(owners // 2 * station_count, full_width),
        ("z_hi", "x"),
        scatter_dimension=0,
        tiled=True,
    )
    return finish(summed, own_spec, band_count)


def solution(mesh):
    fine = jax.sharding.Mesh(
        mesh.devices.reshape(2, 4, 2, 4, 2), ("z_hi", "x", "core", "y", "z_lo")
    )
    pairs = ("z_hi", "x", "core")
    band = ("y", "z_lo")
    return jax.shard_map(
        shards,
        mesh=fine,
        in_specs=(
            P(pairs, band, None),
            P(pairs, band, None),
            P(pairs, None),
            P(pairs, None),
            P(pairs),
            P(pairs),
        ),
        out_specs=P(pairs, band, None),
        check_vma=False,
    )
```

```python
import math

import jax
import jax.numpy as jnp
from jax import lax
from jax.sharding import PartitionSpec as P
from jax.experimental import pallas as pl
from jax.experimental.pallas import tpu as pltpu


def lag_basis(half_width, lag_count):
    freqs = jnp.arange(half_width, dtype=jnp.int32)
    lag_index = jnp.arange(lag_count, dtype=jnp.int32)
    phases = (freqs[:, None] * lag_index[None, :] % lag_count).astype(jnp.float32) * (
        2.0 * math.pi / lag_count
    )
    factor = 1.0 / math.sqrt(lag_count)
    return jnp.concatenate([jnp.cos(phases) * factor, -jnp.sin(phases) * factor], axis=0).astype(
        jnp.bfloat16
    )


def owner_positions(owner_flat, owner_count):
    onehot = (owner_flat[:, None] == jnp.arange(owner_count, dtype=jnp.int32)[None, :]).astype(
        jnp.int32
    )
    before = jnp.cumsum(onehot, axis=0) - onehot
    return jnp.sum(before * onehot, axis=1)


def round_bf16(x):
    return x.astype(jnp.bfloat16).astype(jnp.float32)


def pair_kernel(near_ref, far_ref, ns_ref, fs_ref, obs_ref, ws_ref, we_ref, table_ref, out_ref):
    half = near_ref.shape[1] // 2
    near = round_bf16(near_ref[...].astype(jnp.float32) * ns_ref[...])
    far = round_bf16(far_ref[...].astype(jnp.float32) * fs_ref[...])
    near_re, near_im = near[:, :half], near[:, half:]
    far_re, far_im = far[:, :half], far[:, half:]
    cross_re = (near_re * far_re + near_im * far_im).astype(jnp.bfloat16)
    cross_im = (near_im * far_re - near_re * far_im).astype(jnp.bfloat16)
    tab_re = table_ref[:half, :]
    tab_im = table_ref[half:, :]
    lagged = jnp.dot(cross_re, tab_re, preferred_element_type=jnp.float32) + jnp.dot(
        cross_im, tab_im, preferred_element_type=jnp.float32
    )
    lag = lax.broadcasted_iota(jnp.int32, lagged.shape, 1)
    inside = (lag >= ws_ref[...]) & (lag < we_ref[...])
    residual = jnp.where(inside, lagged - obs_ref[...].astype(jnp.float32), 0.0).astype(
        jnp.bfloat16
    )
    dims = (((1,), (1,)), ((), ()))
    adj_re = lax.dot_general(residual, tab_re, dims, preferred_element_type=jnp.float32)
    adj_im = lax.dot_general(residual, tab_im, dims, preferred_element_type=jnp.float32)
    out_ref[0, :, :half] = (adj_re * far_re - adj_im * far_im).astype(jnp.bfloat16)
    out_ref[0, :, half:] = (adj_re * far_im + adj_im * far_re).astype(jnp.bfloat16)
    out_ref[1, :, :half] = (adj_re * near_re + adj_im * near_im).astype(jnp.bfloat16)
    out_ref[1, :, half:] = (adj_re * near_im - adj_im * near_re).astype(jnp.bfloat16)


def pair_contributions(near_raw, far_raw, near_scale, far_scale, obs, ws, we, table, block=512):
    pairs, width = near_raw.shape
    lags = obs.shape[1]
    row = lambda i: (i, 0)
    return pl.pallas_call(
        pair_kernel,
        grid=(pairs // block,),
        in_specs=[
            pl.BlockSpec((block, width), row),
            pl.BlockSpec((block, width), row),
            pl.BlockSpec((block, 1), row),
            pl.BlockSpec((block, 1), row),
            pl.BlockSpec((block, lags), row),
            pl.BlockSpec((block, 1), row),
            pl.BlockSpec((block, 1), row),
            pl.BlockSpec((width, lags), lambda i: (0, 0)),
        ],
        out_specs=pl.BlockSpec((2, block, width), lambda i: (0, i, 0)),
        out_shape=jax.ShapeDtypeStruct((2, pairs, width), jnp.bfloat16),
        compiler_params=pltpu.CompilerParams(vmem_limit_bytes=48 * 1024 * 1024),
    )(near_raw, far_raw, near_scale, far_scale, obs, ws, we, table)


def finish_kernel(summed_ref, own_ref, out_ref):
    half = own_ref.shape[1] // 2
    summed = summed_ref[...].astype(jnp.float32)
    own = own_ref[...]
    value = 0.25 * (summed[:, :half] * own[:, :half] + summed[:, half:] * own[:, half:])
    out_ref[...] = value.reshape(out_ref.shape)


def finish(summed, own_spec, band_count):
    stations, width = own_spec.shape
    return pl.pallas_call(
        finish_kernel,
        out_shape=jax.ShapeDtypeStruct((stations, band_count, width // 2), jnp.float32),
    )(summed, own_spec)


def shards(spectra, observed, pair_owner, pair_slot, win_start, win_end):
    owners = lax.axis_size(("z_hi", "x", "core"))
    station_count = spectra.shape[0]
    band_count = spectra.shape[1]
    full_width = spectra.shape[2]
    half_width = full_width // 2
    pair_count = observed.shape[0]
    lag_count = observed.shape[2]
    capacity = 3 * pair_count // owners
    raw = spectra.reshape(station_count, full_width)
    panel_raw = lax.all_gather(raw, ("z_hi", "x", "core"), axis=0, tiled=True)
    spectrum = raw.astype(jnp.float32)
    local_power = jnp.sum(spectrum * spectrum, axis=1)
    total_power = lax.psum(local_power, ("y", "z_lo"))
    entries = band_count * lax.axis_size(("y", "z_lo")) * full_width
    scale = lax.rsqrt(total_power / entries + 1e-05)
    own_spec = lax.reduce_precision(spectrum * scale[:, None], exponent_bits=8, mantissa_bits=7)
    panel_scale = lax.all_gather(scale, ("z_hi", "x", "core"), axis=0, tiled=True)

    rows0 = pair_owner[:, 0] * station_count + pair_slot[:, 0]
    rows1 = pair_owner[:, 1] * station_count + pair_slot[:, 1]
    near_raw = panel_raw[rows0]
    far_raw = panel_raw[rows1]
    near_scale = panel_scale[rows0][:, None]
    far_scale = panel_scale[rows1][:, None]
    table = lag_basis(half_width, lag_count)
    obs = observed.reshape(pair_count, lag_count)
    contribs = pair_contributions(
        near_raw, far_raw, near_scale, far_scale, obs,
        win_start[:, None], win_end[:, None], table,
    ).reshape(2 * pair_count, full_width)
    core = lax.axis_index("core")
    owner_flat = jnp.concatenate([pair_owner[:, 0], pair_owner[:, 1]])
    owner_flat = ((owner_flat % 2) ^ core) * (owners // 2) + owner_flat // 2
    slot_flat = jnp.concatenate([pair_slot[:, 0], pair_slot[:, 1]])
    position = owner_positions(owner_flat, owners)
    flat_slot = owner_flat * capacity + position
    slot_station = (
        jnp.full((owners * capacity,), station_count, jnp.int32)
        .at[flat_slot]
        .set(slot_flat, unique_indices=True)
    ).reshape(owners, 1, capacity)
    slotted = (
        jnp.zeros((owners * capacity, full_width), jnp.bfloat16)
        .at[flat_slot]
        .set(contribs, unique_indices=True)
    ).reshape(owners, capacity, full_width)
    station_ids = jnp.arange(station_count, dtype=jnp.int32)[None, :, None]
    onehot = (slot_station == station_ids).astype(jnp.bfloat16)
    half = owners // 2
    quarter = half // 4
    taken = []
    for start in range(half, owners, quarter):
        give = jnp.einsum(
            "osk,okf->osf",
            onehot[start:start + quarter],
            slotted[start:start + quarter],
            preferred_element_type=jnp.float32,
        ).astype(jnp.bfloat16)
        taken.append(lax.ppermute(give, "core", perm=[(0, 1), (1, 0)]))
    chip_sum = []
    for part, start in enumerate(range(0, half, 2 * quarter)):
        keep = jnp.einsum(
            "osk,okf->osf",
            onehot[start:start + 2 * quarter],
            slotted[start:start + 2 * quarter],
            preferred_element_type=jnp.float32,
        )
        arrived = jnp.concatenate(taken[2 * part:2 * part + 2], axis=0)
        chip_sum.append((keep + arrived.astype(jnp.float32)).astype(jnp.bfloat16))
    chip_sum = jnp.concatenate(chip_sum, axis=0)
    summed = lax.psum_scatter(
        chip_sum.reshape(owners // 2 * station_count, full_width),
        ("z_hi", "x"),
        scatter_dimension=0,
        tiled=True,
    )
    return finish(summed, own_spec, band_count)


def solution(mesh):
    fine = jax.sharding.Mesh(
        mesh.devices.reshape(2, 4, 2, 4, 2), ("z_hi", "x", "core", "y", "z_lo")
    )
    pairs = ("z_hi", "x", "core")
    band = ("y", "z_lo")
    return jax.shard_map(
        shards,
        mesh=fine,
        in_specs=(
            P(pairs, band, None),
            P(pairs, band, None),
            P(pairs, None),
            P(pairs, None),
            P(pairs),
            P(pairs),
        ),
        out_specs=P(pairs, band, None),
        check_vma=False,
    )
```
